256 devices in a mesh: gx: 32 (over z, x), gy: 8 (over y, core).
Axes of the slice: x: 4, y: 4, z: 8, core: 2. Of those that a mesh axis runs over, the one named last changes fastest.
Arguments:
- hidden_in: bfloat16 [64, 5120], P(None, 'gx'), may hold values from -60 to 60
- norm1_gain: float32 [5120], P('gx'), may hold values from 0.1 to 1.9
- norm1_bias: float32 [5120], P('gx'), may hold values from -4 to 4
- norm2_gain: float32 [5120], P('gx'), may hold values from 0.1 to 1.9
- norm2_bias: float32 [5120], P('gx'), may hold values from -4 to 4
- w_qkv: bfloat16 [5120, 15360], P('gx', 'gy'), may hold values from -0.078125 to 0.078125
- b_qkv: float32 [15360], P('gy'), may hold values from -4 to 4
- w_out: bfloat16 [5120, 5120], P('gy', 'gx'), may hold values from -0.078125 to 0.078125
- b_out: float32 [5120], P('gx'), may hold values from -4 to 4
- w_up: bfloat16 [5120, 20480], P('gx', 'gy'), may hold values from -0.078125 to 0.078125
- b_up: float32 [20480], P('gy'), may hold values from -4 to 4
- w_down: bfloat16 [20480, 5120], P('gy', 'gx'), may hold values from -0.0390625 to 0.0390625
- b_down: float32 [5120], P('gx'), may hold values from -4 to 4
- key_cache: bfloat16 [64, 40, 1024, 128], P('gx', 'gy'), may hold values from -70 to 70
- value_cache: bfloat16 [64, 40, 1024, 128], P('gx', 'gy'), may hold values from -6 to 6
- lengths: int32 [64], replicated, may hold values from 1 to 1024, 32768 in all
- assignment: int32 [64], replicated, may hold values from 0 to 63, each once
Outputs:
- hidden_out: bfloat16 [64, 5120], P(None, 'gx')
- new_keys: bfloat16 [64, 40, 1024, 128], P('gx', 'gy')
- new_values: bfloat16 [64, 40, 1024, 128], P('gx', 'gy')
The draws below stay inside these ranges and needn't reach their ends.
Inputs may be any that keep to these rules, and one draw needn't show every extreme that they name: `lengths`: each request's length, the largest exactly 1024. `assignment`: a permutation: every slot holds exactly one request.
All inputs are finite; a program needn't handle non-finite values.
Results may differ from the reference program's by a relative error of at most 0.0068.
Values may be sent and summed in bfloat16 or wider, within the bound.
No kernel may reach another device: no remote copies, remote signals or barrier semaphores. Data moves between devices by JAX's collectives and lax.ppermute only.
A program may use at most 64 MiB of HBM per device.

```python
import math
import jax
import jax.numpy as jnp
import numpy as np
from jax import lax

D = 5120
HEADS = 40
HD = 128
FF = 20480
ROT = 32
MAXLEN = 1024
REQUESTS = 64


def draw_hidden_in(key, part):
    first_key = jax.random.fold_in(jax.random.fold_in(key, 11), 0)
    ramp = 0.5 + 1.5 * jnp.arange(D, dtype=jnp.float32) / D
    base = jnp.clip(jax.random.normal(first_key, (REQUESTS, D), jnp.float32), -6.0, 6.0)
    return (base * ramp).astype(jnp.bfloat16)


def draw_key_cache(key, part):
    first_key = jax.random.fold_in(jax.random.fold_in(key, 23), 0)
    shape = (REQUESTS, HEADS, MAXLEN, HD)
    base = jnp.clip(jax.random.normal(first_key, shape, jnp.float32), -6.0, 6.0)
    return base.astype(jnp.bfloat16)


def block_levels(key, extent, shards, low, top_value):
    def one(dim, blocks):
        heights = jax.random.uniform(jax.random.fold_in(jax.random.fold_in(key, 6), dim), (blocks,), jnp.float32, low / len(shards), top_value / len(shards))
        return jnp.repeat(jnp.exp(heights), extent[dim] // blocks).reshape((-1,) + (1,) * (len(extent) - dim - 1))

    factor_of = one(*shards[0])
    for cut in shards[1:]:
        factor_of = factor_of * one(*cut)
    return factor_of


def split_up(amount, total, most, slope):
    weights = [(1 << 20) // math.isqrt(rank ** slope) + 1 for rank in range(2, amount + 1)]
    rest, counts = total - most - (amount - 1), [1] * (amount - 1)
    while rest > 0:
        free = [i for i in range(amount - 1) if counts[i] < most]
        mass, remaining = sum([weights[i] for i in free]), rest
        for i in free:
            extra = min(most - counts[i], max(1, remaining * weights[i] // mass), rest)
            counts[i] = counts[i] + extra
            rest = rest - extra
    return np.array([most] + counts)


def ragged(key, count, total, limit, slope):
    if count == 2:
        one = jax.random.randint(key, (), max(1, total - limit), min(limit, total - 1) + 1)
        return jnp.stack([one, total - one])
    sizes = jnp.asarray(split_up(count, total, limit, slope), jnp.int32)
    pairs = (count - 1) // 2
    giver, taker = sizes[1:1 + 2 * pairs:2], sizes[2:2 + 2 * pairs:2]
    margin = jnp.minimum(giver - 1, limit - taker)
    shifted = jax.random.randint(jax.random.fold_in(key, 1), (pairs,), 0, 1 << 20) % (margin + 1)
    sizes = sizes.at[1:1 + 2 * pairs:2].set(giver - shifted).at[2:2 + 2 * pairs:2].set(taker + shifted)
    return sizes[jax.random.permutation(jax.random.fold_in(key, 2), count)]


def gaussian(own_key, extent, width, most, shards=(), kind=jnp.bfloat16):
    drawn = width * jax.random.normal(own_key, extent, jnp.float32)
    if shards:
        drawn = drawn * block_levels(own_key, extent, shards, -0.22, 0.18)
    return jnp.clip(drawn, -most, most).astype(kind)


def setup_inputs(seed: int = 0) -> dict:
    streams_of = jax.random.split(jax.random.key(seed), 18)
    hidden_in = draw_hidden_in(jax.random.fold_in(streams_of[17], 71), 0)
    norm1_gain = jnp.clip(1.0 + 0.18 * jax.random.normal(streams_of[1], (D,), jnp.float32), 0.1, 1.9)
    norm1_bias = gaussian(streams_of[2], (D,), 0.3, 4.0, ((0, 32),), jnp.float32)
    norm2_gain = jnp.clip(1.0 + 0.18 * jax.random.normal(streams_of[3], (D,), jnp.float32), 0.1, 1.9)
    norm2_bias = gaussian(streams_of[4], (D,), 0.3, 4.0, ((0, 32),), jnp.float32)
    w_qkv = gaussian(streams_of[5], (D, 3 * D), D ** -0.5, 0.078125, ((0, 32), (1, 8)))
    b_qkv = gaussian(streams_of[6], (3 * D,), 0.5, 4.0, ((0, 8),), jnp.float32)
    w_out = gaussian(streams_of[7], (D, D), D ** -0.5, 0.078125, ((0, 8), (1, 32)))
    b_out = gaussian(streams_of[8], (D,), 0.5, 4.0, ((0, 32),), jnp.float32)
    w_up = gaussian(streams_of[9], (D, FF), D ** -0.5, 0.078125, ((0, 32), (1, 8)))
    b_up = gaussian(streams_of[10], (FF,), 0.5, 4.0, ((0, 8),), jnp.float32)
    w_down = gaussian(streams_of[11], (FF, D), FF ** -0.5, 0.0390625, ((0, 8), (1, 32)))
    b_down = gaussian(streams_of[12], (D,), 0.5, 4.0, ((0, 32),), jnp.float32)
    key_cache = draw_key_cache(jax.random.fold_in(streams_of[17], 71), 0)
    value_cache = gaussian(streams_of[14], (REQUESTS, HEADS, MAXLEN, HD), 1.0, 6.0, ((0, 32), (1, 8)))
    lengths = ragged(streams_of[15], REQUESTS, REQUESTS * MAXLEN // 2, MAXLEN, 2).astype(jnp.int32)
    assignment = jax.random.permutation(streams_of[16], REQUESTS).astype(jnp.int32)
    return {"hidden_in": hidden_in, "norm1_gain": norm1_gain, "norm1_bias": norm1_bias, "norm2_gain": norm2_gain, "norm2_bias": norm2_bias, "w_qkv": w_qkv, "b_qkv": b_qkv, "w_out": w_out, "b_out": b_out, "w_up": w_up, "b_up": b_up, "w_down": w_down, "b_down": b_down, "key_cache": key_cache, "value_cache": value_cache, "lengths": lengths, "assignment": assignment}


def rotate(tensor, position):
    half_rot = ROT // 2
    frequency = 10000.0 ** (-2.0 * jnp.arange(half_rot, dtype=jnp.float32) / ROT)
    angle = position.astype(jnp.float32)[:, None, None] * frequency
    cosine = jnp.cos(angle)
    sine = jnp.sin(angle)
    first_half = tensor[..., :half_rot]
    second_half = tensor[..., half_rot:ROT]
    return jnp.concatenate([first_half * cosine - second_half * sine, second_half * cosine + first_half * sine, tensor[..., ROT:]], axis=-1)

def reference(hidden_in, norm1_gain, norm1_bias, norm2_gain, norm2_bias, w_qkv, b_qkv, w_out, b_out, w_up, b_up, w_down, b_down, key_cache, value_cache, lengths, assignment):
    wide_in = hidden_in.astype(jnp.float32)
    row_mean = lax.optimization_barrier(jnp.sum(wide_in, axis=1)) / D
    row_var = lax.optimization_barrier(jnp.sum(wide_in * wide_in, axis=1)) / D - row_mean * row_mean
    normed = (wide_in - row_mean[:, None]) * lax.rsqrt(row_var + 1e-05)[:, None]
    attn_in = (normed * norm1_gain + norm1_bias).astype(jnp.bfloat16)
    mlp_in = (normed * norm2_gain + norm2_bias).astype(jnp.bfloat16)
    qkv = jnp.dot(attn_in, w_qkv, preferred_element_type=jnp.float32) + b_qkv
    qkv = qkv.reshape(REQUESTS, HEADS, 3, HD)
    position = lengths - 1
    query = rotate(qkv[:, :, 0], position).astype(jnp.bfloat16)
    new_key = rotate(qkv[:, :, 1], position).astype(jnp.bfloat16)
    new_value = qkv[:, :, 2].astype(jnp.bfloat16)
    new_keys = key_cache.at[assignment, :, position, :].set(new_key)
    new_values = value_cache.at[assignment, :, position, :].set(new_value)
    scale = HD ** (-0.5)

    def attend_one(items):
        query_row, slot_id, length = items
        keys = lax.dynamic_index_in_dim(new_keys, slot_id, 0, keepdims=False).astype(jnp.float32)
        values = lax.dynamic_index_in_dim(new_values, slot_id, 0, keepdims=False).astype(jnp.float32)
        scores = jnp.einsum('hd,hpd->hp', query_row.astype(jnp.float32), keys) * scale
        valid = jnp.arange(MAXLEN, dtype=jnp.int32)[None, :] < length
        scores = jnp.where(valid, scores, -1e+30)
        top_score = lax.optimization_barrier(jnp.max(scores, axis=1))
        weights = jnp.where(valid, jnp.exp(scores - top_score[:, None]), 0.0)
        total = lax.optimization_barrier(jnp.sum(weights, axis=1))
        weights_low = lax.optimization_barrier(weights.astype(jnp.bfloat16))
        weighted = jnp.einsum('hp,hpd->hd', weights_low.astype(jnp.float32), values)
        return (weighted / total[:, None]).astype(jnp.bfloat16)
    attended = lax.map(attend_one, (query, assignment, lengths)).reshape(REQUESTS, D)
    attn_part = jnp.dot(attended, w_out, preferred_element_type=jnp.float32)
    up = jnp.dot(mlp_in, w_up, preferred_element_type=jnp.float32) + b_up
    hidden = jax.nn.gelu(up, approximate=False).astype(jnp.bfloat16)
    mlp_part = jnp.dot(hidden, w_down, preferred_element_type=jnp.float32)
    hidden_out = (wide_in + attn_part + mlp_part + b_out + b_down).astype(jnp.bfloat16)
    return (hidden_out, new_keys, new_values)
```

```python
import functools

import jax
import jax.numpy as jnp
from jax import lax
from jax.sharding import PartitionSpec as P

D = 5120
HD = 128
ROT = 32


def rotate(tensor, position):
    half_rot = ROT // 2
    frequency = 10000.0 ** (-2.0 * jnp.arange(half_rot, dtype=jnp.float32) / ROT)
    angle = position.astype(jnp.float32)[:, None, None] * frequency
    cosine = jnp.cos(angle)
    sine = jnp.sin(angle)
    first_half = tensor[..., :half_rot]
    second_half = tensor[..., half_rot:ROT]
    return jnp.concatenate(
        [
            first_half * cosine - second_half * sine,
            second_half * cosine + first_half * sine,
            tensor[..., ROT:],
        ],
        axis=-1,
    )


def block_scores(query, keys, my_len):
    span_len = keys.shape[2]
    scores = jnp.einsum("shd,shpd->shp", query, keys, preferred_element_type=jnp.float32) * HD ** (
        -0.5
    )
    places = lax.iota(jnp.int32, span_len)
    valid = places[None, None, :] < my_len[:, None, None]
    return (jnp.where(valid, scores, -1e30), valid)


def xor_pairs(size, bit):
    return [(i, i ^ (1 << bit)) for i in range(size)]


def tree_sum(x, axis, size, bits):
    for bit in bits:
        x = x + lax.ppermute(x, axis, xor_pairs(size, bit))
    return x


def tree_scatter_sum(x, axis, size, bits):
    rows = x.shape[0]
    me = lax.axis_index(axis)
    x = x.reshape((2,) * len(bits) + (rows // size,) + x.shape[1:])
    left = list(range(len(bits) - 1, -1, -1))
    for bit in bits:
        at = left.index(bit)
        mine = (me >> bit) & 1
        keep = lax.dynamic_index_in_dim(x, mine, at, keepdims=False)
        send = lax.dynamic_index_in_dim(x, 1 - mine, at, keepdims=False)
        x = keep + lax.ppermute(send, axis, xor_pairs(size, bit))
        left.pop(at)
    return x.reshape((rows // size,) + x.shape[-1:])


def tree_gather(x, axis, size, bits):
    me = lax.axis_index(axis)
    held = []
    for bit in bits:
        other = lax.ppermute(x, axis, xor_pairs(size, bit))
        low = (me >> bit) & 1 == 0
        x = jnp.stack([jnp.where(low, x, other), jnp.where(low, other, x)], 0)
        held.insert(0, bit)
    count = len(bits)
    order = [held.index(bit) for bit in range(count - 1, -1, -1)]
    x = jnp.transpose(x, order + list(range(count, x.ndim)))
    return x.reshape((size * x.shape[count],) + x.shape[count + 1 :])


def bit_order(size, first):
    bits = [b for b in first if (1 << b) < size]
    return bits + [b for b in range(size.bit_length() - 1) if b not in bits]


def on_device(
    hidden_in,
    norm1_gain,
    norm1_bias,
    norm2_gain,
    norm2_bias,
    w_qkv,
    b_qkv,
    w_out,
    b_out,
    w_up,
    b_up,
    w_down,
    b_down,
    key_cache,
    value_cache,
    lengths,
    assignment,
    gx_size,
    gy_size,
):
    requests = hidden_in.shape[0]
    rows_dev = key_cache.shape[0]
    heads_dev = key_cache.shape[1]
    gx_bits = bit_order(gx_size, (0, 2, 1, 3, 4))
    gy_bits = bit_order(gy_size, (0, 1, 2))
    wide_in = hidden_in.astype(jnp.float32)
    stats = tree_sum(
        jnp.stack([jnp.sum(wide_in, axis=1), jnp.sum(wide_in * wide_in, axis=1)]),
        "gx",
        gx_size,
        gx_bits,
    )
    sum_rows, sum_squares = stats[0], stats[1]
    row_mean = sum_rows / D
    row_var = sum_squares / D - row_mean * row_mean
    normed = (wide_in - row_mean[:, None]) * lax.rsqrt(row_var + 1e-05)[:, None]
    attn_in = (normed * norm1_gain + norm1_bias).astype(jnp.bfloat16)
    mlp_in = (normed * norm2_gain + norm2_bias).astype(jnp.bfloat16)
    slot_ids = lax.iota(jnp.int32, requests)
    matches = assignment[:, None] == slot_ids[None, :]
    to_request = matches.astype(jnp.float32)
    to_slot = matches.T.astype(jnp.bfloat16)
    attn_slot = jnp.dot(to_slot, attn_in, preferred_element_type=jnp.float32).astype(jnp.bfloat16)
    mlp_slot = jnp.dot(to_slot, mlp_in, preferred_element_type=jnp.float32).astype(jnp.bfloat16)
    slot_len = jnp.sum(jnp.where(matches, lengths[:, None], 0), axis=0)
    my_len = lax.dynamic_slice_in_dim(slot_len, lax.axis_index("gx") * rows_dev, rows_dev, 0)
    qkv_cols = w_qkv.shape[1]
    partial = jnp.concatenate(
        [
            jnp.dot(attn_slot, w_qkv, preferred_element_type=jnp.float32),
            jnp.dot(mlp_slot, w_up, preferred_element_type=jnp.float32),
        ],
        axis=1,
    )
    reduced = tree_scatter_sum(partial, "gx", gx_size, gx_bits)
    qkv = reduced[:, :qkv_cols] + b_qkv
    up = reduced[:, qkv_cols:] + b_up
    qkv = qkv.reshape(rows_dev, heads_dev, 3, HD)
    position = my_len - 1
    query = rotate(qkv[:, :, 0], position).astype(jnp.bfloat16)
    new_key = rotate(qkv[:, :, 1], position).astype(jnp.bfloat16)
    new_value = qkv[:, :, 2].astype(jnp.bfloat16)
    new_keys = key_cache
    new_values = value_cache
    zero_index = jnp.int32(0)
    for local_slot in range(rows_dev):
        slot_index = jnp.int32(local_slot)
        new_keys = lax.dynamic_update_slice(
            new_keys,
            new_key[local_slot][None, :, None, :],
            (slot_index, zero_index, position[local_slot], zero_index),
        )
        new_values = lax.dynamic_update_slice(
            new_values,
            new_value[local_slot][None, :, None, :],
            (slot_index, zero_index, position[local_slot], zero_index),
        )
    scores, valid = block_scores(query, new_keys, my_len)
    top_score = jnp.max(scores, axis=2)
    weights = jnp.where(valid, jnp.exp(scores - top_score[:, :, None]), 0.0)
    total = jnp.sum(weights, axis=2)
    weights_low = weights.astype(jnp.bfloat16)
    weighted = jnp.einsum(
        "shp,shpd->shd", weights_low, new_values, preferred_element_type=jnp.float32
    )
    attended = (weighted / total[:, :, None]).astype(jnp.bfloat16).reshape(rows_dev, heads_dev * HD)
    hidden = jax.nn.gelu(up, approximate=False).astype(jnp.bfloat16)
    gathered = tree_gather(
        jnp.concatenate([attended, hidden], axis=1), "gx", gx_size, gx_bits[::-1]
    )
    attn_cols = attended.shape[1]
    slot_part = jnp.dot(
        gathered[:, :attn_cols], w_out, preferred_element_type=jnp.float32
    ) + jnp.dot(gathered[:, attn_cols:], w_down, preferred_element_type=jnp.float32)
    branches = tree_sum(slot_part, "gy", gy_size, gy_bits)
    branches = jnp.dot(to_request, branches, precision=lax.Precision.HIGHEST)
    hidden_out = (wide_in + branches + b_out + b_down).astype(jnp.bfloat16)
    return (hidden_out, new_keys, new_values)


def solution(mesh):
    body = functools.partial(on_device, gx_size=mesh.shape["gx"], gy_size=mesh.shape["gy"])
    return jax.shard_map(
        body,
        mesh=mesh,
        in_specs=(
            P(None, "gx"),
            P("gx"),
            P("gx"),
            P("gx"),
            P("gx"),
            P("gx", "gy"),
            P("gy"),
            P("gy", "gx"),
            P("gx"),
            P("gx", "gy"),
            P("gy"),
            P("gy", "gx"),
            P("gx"),
            P("gx", "gy", None, None),
            P("gx", "gy", None, None),
            P(),
            P(),
        ),
        out_specs=(P(None, "gx"), P("gx", "gy", None, None), P("gx", "gy", None, None)),
        check_vma=False,
    )
```

```python
import functools

import jax
import jax.numpy as jnp
from jax import lax
from jax.sharding import PartitionSpec as P

D = 5120
HD = 128
ROT = 32


def rotate(tensor, position):
    half_rot = ROT // 2
    frequency = 10000.0 ** (-2.0 * jnp.arange(half_rot, dtype=jnp.float32) / ROT)
    angle = position.astype(jnp.float32)[:, None, None] * frequency
    cosine = jnp.cos(angle)
    sine = jnp.sin(angle)
    first_half = tensor[..., :half_rot]
    second_half = tensor[..., half_rot:ROT]
    return jnp.concatenate(
        [
            first_half * cosine - second_half * sine,
            second_half * cosine + first_half * sine,
            tensor[..., ROT:],
        ],
        axis=-1,
    )


def block_scores(query, keys, my_len):
    span_len = keys.shape[2]
    scores = jnp.einsum("shd,shpd->shp", query, keys, preferred_element_type=jnp.float32) * HD ** (
        -0.5
    )
    places = lax.iota(jnp.int32, span_len)
    valid = places[None, None, :] < my_len[:, None, None]
    return (jnp.where(valid, scores, -1e30), valid)


def xor_pairs(size, bit):
    return [(i, i ^ (1 << bit)) for i in range(size)]


def tree_sum(x, axis, size, bits):
    for bit in bits:
        x = x + lax.ppermute(x, axis, xor_pairs(size, bit))
    return x


def tree_scatter_sum(x, axis, size, bits):
    rows = x.shape[0]
    me = lax.axis_index(axis)
    x = x.reshape((2,) * len(bits) + (rows // size,) + x.shape[1:])
    left = list(range(len(bits) - 1, -1, -1))
    for bit in bits:
        at = left.index(bit)
        mine = (me >> bit) & 1
        keep = lax.dynamic_index_in_dim(x, mine, at, keepdims=False)
        send = lax.dynamic_index_in_dim(x, 1 - mine, at, keepdims=False)
        x = keep + lax.ppermute(send, axis, xor_pairs(size, bit))
        left.pop(at)
    return x.reshape((rows // size,) + x.shape[-1:])


def tree_gather(x, axis, size, bits):
    me = lax.axis_index(axis)
    held = []
    for bit in bits:
        other = lax.ppermute(x, axis, xor_pairs(size, bit))
        low = (me >> bit) & 1 == 0
        x = jnp.stack([jnp.where(low, x, other), jnp.where(low, other, x)], 0)
        held.insert(0, bit)
    count = len(bits)
    order = [held.index(bit) for bit in range(count - 1, -1, -1)]
    x = jnp.transpose(x, order + list(range(count, x.ndim)))
    return x.reshape((size * x.shape[count],) + x.shape[count + 1 :])


def exchange_sum(x, axis, size):
    spread = jnp.broadcast_to(x[None], (size,) + x.shape)
    return jnp.sum(lax.all_to_all(spread, axis, 0, 0, tiled=False), axis=0)


def exchange_scatter_sum(x, axis, size):
    blocks = x.reshape((size, x.shape[0] // size) + x.shape[1:])
    return jnp.sum(lax.all_to_all(blocks, axis, 0, 0, tiled=False), axis=0)


def exchange_gather(x, axis, size):
    spread = jnp.broadcast_to(x[None], (size,) + x.shape)
    out = lax.all_to_all(spread, axis, 0, 0, tiled=False)
    return out.reshape((size * x.shape[0],) + x.shape[1:])


def bit_order(size, first):
    bits = [b for b in first if (1 << b) < size]
    return bits + [b for b in range(size.bit_length() - 1) if b not in bits]


def on_device(
    hidden_in,
    norm1_gain,
    norm1_bias,
    norm2_gain,
    norm2_bias,
    w_qkv,
    b_qkv,
    w_out,
    b_out,
    w_up,
    b_up,
    w_down,
    b_down,
    key_cache,
    value_cache,
    lengths,
    assignment,
    gx_size,
    gy_size,
):
    requests = hidden_in.shape[0]
    rows_dev = key_cache.shape[0]
    heads_dev = key_cache.shape[1]
    gx_bits = bit_order(gx_size, (0, 2, 1, 3, 4))
    gy_bits = bit_order(gy_size, (0, 1, 2))
    wide_in = hidden_in.astype(jnp.float32)
    stats = exchange_sum(
        jnp.stack([jnp.sum(wide_in, axis=1), jnp.sum(wide_in * wide_in, axis=1)]),
        "gx",
        gx_size,
    )
    sum_rows, sum_squares = stats[0], stats[1]
    row_mean = sum_rows / D
    row_var = sum_squares / D - row_mean * row_mean
    normed = (wide_in - row_mean[:, None]) * lax.rsqrt(row_var + 1e-05)[:, None]
    attn_in = (normed * norm1_gain + norm1_bias).astype(jnp.bfloat16)
    mlp_in = (normed * norm2_gain + norm2_bias).astype(jnp.bfloat16)
    slot_ids = lax.iota(jnp.int32, requests)
    matches = assignment[:, None] == slot_ids[None, :]
    to_request = matches.astype(jnp.float32)
    to_slot = matches.T.astype(jnp.bfloat16)
    attn_slot = jnp.dot(to_slot, attn_in, preferred_element_type=jnp.float32).astype(jnp.bfloat16)
    mlp_slot = jnp.dot(to_slot, mlp_in, preferred_element_type=jnp.float32).astype(jnp.bfloat16)
    slot_len = jnp.sum(jnp.where(matches, lengths[:, None], 0), axis=0)
    my_len = lax.dynamic_slice_in_dim(slot_len, lax.axis_index("gx") * rows_dev, rows_dev, 0)
    qkv_cols = w_qkv.shape[1]
    partial = jnp.concatenate(
        [
            jnp.dot(attn_slot, w_qkv, preferred_element_type=jnp.float32),
            jnp.dot(mlp_slot, w_up, preferred_element_type=jnp.float32),
        ],
        axis=1,
    )
    reduced = exchange_scatter_sum(partial, "gx", gx_size)
    qkv = reduced[:, :qkv_cols] + b_qkv
    up = reduced[:, qkv_cols:] + b_up
    qkv = qkv.reshape(rows_dev, heads_dev, 3, HD)
    position = my_len - 1
    query = rotate(qkv[:, :, 0], position).astype(jnp.bfloat16)
    new_key = rotate(qkv[:, :, 1], position).astype(jnp.bfloat16)
    new_value = qkv[:, :, 2].astype(jnp.bfloat16)
    new_keys = key_cache
    new_values = value_cache
    zero_index = jnp.int32(0)
    for local_slot in range(rows_dev):
        slot_index = jnp.int32(local_slot)
        new_keys = lax.dynamic_update_slice(
            new_keys,
            new_key[local_slot][None, :, None, :],
            (slot_index, zero_index, position[local_slot], zero_index),
        )
        new_values = lax.dynamic_update_slice(
            new_values,
            new_value[local_slot][None, :, None, :],
            (slot_index, zero_index, position[local_slot], zero_index),
        )
    scores, valid = block_scores(query, new_keys, my_len)
    top_score = jnp.max(scores, axis=2)
    weights = jnp.where(valid, jnp.exp(scores - top_score[:, :, None]), 0.0)
    total = jnp.sum(weights, axis=2)
    weights_low = weights.astype(jnp.bfloat16)
    weighted = jnp.einsum(
        "shp,shpd->shd", weights_low, new_values, preferred_element_type=jnp.float32
    )
    attended = (weighted / total[:, :, None]).astype(jnp.bfloat16).reshape(rows_dev, heads_dev * HD)
    hidden = jax.nn.gelu(up, approximate=False).astype(jnp.bfloat16)
    gathered = exchange_gather(jnp.concatenate([attended, hidden], axis=1), "gx", gx_size)
    attn_cols = attended.shape[1]
    slot_part = jnp.dot(
        gathered[:, :attn_cols], w_out, preferred_element_type=jnp.float32
    ) + jnp.dot(gathered[:, attn_cols:], w_down, preferred_element_type=jnp.float32)
    branches = tree_sum(slot_part, "gy", gy_size, gy_bits)
    branches = jnp.dot(to_request, branches, precision=lax.Precision.HIGHEST)
    hidden_out = (wide_in + branches + b_out + b_down).astype(jnp.bfloat16)
    return (hidden_out, new_keys, new_values)


def solution(mesh):
    body = functools.partial(on_device, gx_size=mesh.shape["gx"], gy_size=mesh.shape["gy"])
    return jax.shard_map(
        body,
        mesh=mesh,
        in_specs=(
            P(None, "gx"),
            P("gx"),
            P("gx"),
            P("gx"),
            P("gx"),
            P("gx", "gy"),
            P("gy"),
            P("gy", "gx"),
            P("gx"),
            P("gx", "gy"),
            P("gy"),
            P("gy", "gx"),
            P("gx"),
            P("gx", "gy", None, None),
            P("gx", "gy", None, None),
            P(),
            P(),
        ),
        out_specs=(P(None, "gx"), P("gx", "gy", None, None), P("gx", "gy", None, None)),
        check_vma=False,
    )
```

```python
import functools

import jax
import jax.numpy as jnp
from jax import lax
from jax.sharding import PartitionSpec as P


D = 5120
HD = 128
ROT = 32


def rotate(tensor, position):
    half_rot = ROT // 2
    frequency = 10000.0 ** (-2.0 * jnp.arange(half_rot, dtype=jnp.float32) / ROT)
    angle = position.astype(jnp.float32)[:, None, None] * frequency
    cosine = jnp.cos(angle)
    sine = jnp.sin(angle)
    first_half = tensor[..., :half_rot]
    second_half = tensor[..., half_rot:ROT]
    return jnp.concatenate(
        [
            first_half * cosine - second_half * sine,
            second_half * cosine + first_half * sine,
            tensor[..., ROT:],
        ],
        axis=-1,
    )


def block_scores(query, keys, my_len):
    span_len = keys.shape[2]
    scores = jnp.einsum("shd,shpd->shp", query, keys, preferred_element_type=jnp.float32) * HD ** (
        -0.5
    )
    places = lax.iota(jnp.int32, span_len)
    valid = places[None, None, :] < my_len[:, None, None]
    return (jnp.where(valid, scores, -1e30), valid)


def xor_pairs(size, bit):
    return [(i, i ^ (1 << bit)) for i in range(size)]


def tree_sum(x, axis, size, bits):
    for bit in bits:
        x = x + lax.ppermute(x, axis, xor_pairs(size, bit))
    return x


def exchange_sum(x, axis, size):
    spread = jnp.broadcast_to(x[None], (size,) + x.shape)
    return jnp.sum(lax.all_to_all(spread, axis, 0, 0, tiled=False), axis=0)


def exchange_scatter_sum(x, axis, size):
    blocks = x.reshape((size, x.shape[0] // size) + x.shape[1:])
    return jnp.sum(lax.all_to_all(blocks, axis, 0, 0, tiled=False), axis=0)


def exchange_gather(x, axis, size):
    spread = jnp.broadcast_to(x[None], (size,) + x.shape)
    out = lax.all_to_all(spread, axis, 0, 0, tiled=False)
    return out.reshape((size * x.shape[0],) + x.shape[1:])


def bit_order(size, first):
    bits = [b for b in first if (1 << b) < size]
    return bits + [b for b in range(size.bit_length() - 1) if b not in bits]


def layer(
    hidden_in,
    norm1_gain,
    norm1_bias,
    norm2_gain,
    norm2_bias,
    w_qkv,
    b_qkv,
    w_out,
    b_out,
    w_up,
    b_up,
    w_down,
    b_down,
    key_cache,
    value_cache,
    lengths,
    assignment,
    gx_size,
    gy_size,
):
    requests = hidden_in.shape[0]
    rows_dev = key_cache.shape[0]
    heads_dev = key_cache.shape[1]
    gy_bits = bit_order(gy_size, (0, 1, 2))
    wide_in = hidden_in.astype(jnp.float32)
    stats = exchange_sum(
        jnp.stack([jnp.sum(wide_in, axis=1), jnp.sum(wide_in * wide_in, axis=1)]),
        "gx",
        gx_size,
    )
    sum_rows, sum_squares = stats[0], stats[1]
    row_mean = sum_rows / D
    row_var = sum_squares / D - row_mean * row_mean
    normed = (wide_in - row_mean[:, None]) * lax.rsqrt(row_var + 1e-05)[:, None]
    attn_in = (normed * norm1_gain + norm1_bias).astype(jnp.bfloat16)
    mlp_in = (normed * norm2_gain + norm2_bias).astype(jnp.bfloat16)
    slot_ids = lax.iota(jnp.int32, requests)
    matches = assignment[:, None] == slot_ids[None, :]
    to_request = matches.astype(jnp.float32)
    to_slot = matches.T.astype(jnp.bfloat16)
    attn_slot = jnp.dot(to_slot, attn_in, preferred_element_type=jnp.float32).astype(jnp.bfloat16)
    mlp_slot = jnp.dot(to_slot, mlp_in, preferred_element_type=jnp.float32).astype(jnp.bfloat16)
    slot_len = jnp.sum(jnp.where(matches, lengths[:, None], 0), axis=0)
    my_len = lax.dynamic_slice_in_dim(slot_len, lax.axis_index("gx") * rows_dev, rows_dev, 0)
    qkv_cols = w_qkv.shape[1]
    partial = jnp.concatenate(
        [
            jnp.dot(attn_slot, w_qkv, preferred_element_type=jnp.float32),
            jnp.dot(mlp_slot, w_up, preferred_element_type=jnp.float32),
        ],
        axis=1,
    )
    reduced = exchange_scatter_sum(partial, "gx", gx_size)
    qkv = reduced[:, :qkv_cols] + b_qkv
    up = reduced[:, qkv_cols:] + b_up
    hidden = jax.nn.gelu(up, approximate=False).astype(jnp.bfloat16)
    hidden_all = exchange_gather(hidden, "gx", gx_size)
    qkv = qkv.reshape(rows_dev, heads_dev, 3, HD)
    position = my_len - 1
    query = rotate(qkv[:, :, 0], position).astype(jnp.bfloat16)
    new_key = rotate(qkv[:, :, 1], position).astype(jnp.bfloat16)
    new_value = qkv[:, :, 2].astype(jnp.bfloat16)
    new_keys = key_cache
    new_values = value_cache
    zero_index = jnp.int32(0)
    for local_slot in range(rows_dev):
        slot_index = jnp.int32(local_slot)
        new_keys = lax.dynamic_update_slice(
            new_keys,
            new_key[local_slot][None, :, None, :],
            (slot_index, zero_index, position[local_slot], zero_index),
        )
        new_values = lax.dynamic_update_slice(
            new_values,
            new_value[local_slot][None, :, None, :],
            (slot_index, zero_index, position[local_slot], zero_index),
        )
    scores, valid = block_scores(query, new_keys, my_len)
    top_score = jnp.max(scores, axis=2)
    weights = jnp.where(valid, jnp.exp(scores - top_score[:, :, None]), 0.0)
    total = jnp.sum(weights, axis=2)
    weights_low = weights.astype(jnp.bfloat16)
    weighted = jnp.einsum(
        "shp,shpd->shd", weights_low, new_values, preferred_element_type=jnp.float32
    )
    attended = (weighted / total[:, :, None]).astype(jnp.bfloat16).reshape(rows_dev, heads_dev * HD)
    attended_all = exchange_gather(attended, "gx", gx_size)
    mlp_part = lax.optimization_barrier(
        jnp.dot(hidden_all, w_down, preferred_element_type=jnp.float32)
    )
    slot_part = jnp.dot(attended_all, w_out, preferred_element_type=jnp.float32) + mlp_part
    branches = tree_sum(slot_part, "gy", gy_size, gy_bits)
    branches = jnp.dot(to_request, branches, precision=lax.Precision.HIGHEST)
    hidden_out = (wide_in + branches + b_out + b_down).astype(jnp.bfloat16)
    return (hidden_out, new_keys, new_values)


def solution(mesh):
    body = functools.partial(layer, gx_size=mesh.shape["gx"], gy_size=mesh.shape["gy"])
    return jax.shard_map(
        body,
        mesh=mesh,
        in_specs=(
            P(None, "gx"),
            P("gx"),
            P("gx"),
            P("gx"),
            P("gx"),
            P("gx", "gy"),
            P("gy"),
            P("gy", "gx"),
            P("gx"),
            P("gx", "gy"),
            P("gy"),
            P("gy", "gx"),
            P("gx"),
            P("gx", "gy", None, None),
            P("gx", "gy", None, None),
            P(),
            P(),
        ),
        out_specs=(P(None, "gx"), P("gx", "gy", None, None), P("gx", "gy", None, None)),
        check_vma=False,
    )
```

```python
import functools

import jax
import jax.numpy as jnp
from jax import lax
from jax.sharding import PartitionSpec as P

D = 5120
HD = 128
ROT = 32


def rotate(tensor, position):
    half_rot = ROT // 2
    frequency = 10000.0 ** (-2.0 * jnp.arange(half_rot, dtype=jnp.float32) / ROT)
    angle = position.astype(jnp.float32)[:, None, None] * frequency
    cosine = jnp.cos(angle)
    sine = jnp.sin(angle)
    first_half = tensor[..., :half_rot]
    second_half = tensor[..., half_rot:ROT]
    return jnp.concatenate(
        [
            first_half * cosine - second_half * sine,
            second_half * cosine + first_half * sine,
            tensor[..., ROT:],
        ],
        axis=-1,
    )


def block_scores(query, keys, my_len):
    span_len = keys.shape[2]
    scores = jnp.einsum("shd,shpd->shp", query, keys, preferred_element_type=jnp.float32) * HD ** (
        -0.5
    )
    places = lax.iota(jnp.int32, span_len)
    valid = places[None, None, :] < my_len[:, None, None]
    return (jnp.where(valid, scores, -1e30), valid)


def xor_pairs(size, bit):
    return [(i, i ^ (1 << bit)) for i in range(size)]


def tree_sum(x, axis, size, bits):
    for bit in bits:
        x = x + lax.ppermute(x, axis, xor_pairs(size, bit))
    return x


def tree_scatter_sum(x, axis, size, bits):
    rows = x.shape[0]
    me = lax.axis_index(axis)
    x = x.reshape((2,) * len(bits) + (rows // size,) + x.shape[1:])
    left = list(range(len(bits) - 1, -1, -1))
    for bit in bits:
        at = left.index(bit)
        mine = (me >> bit) & 1
        keep = lax.dynamic_index_in_dim(x, mine, at, keepdims=False)
        send = lax.dynamic_index_in_dim(x, 1 - mine, at, keepdims=False)
        x = keep + lax.ppermute(send, axis, xor_pairs(size, bit))
        left.pop(at)
    return x.reshape((rows // size,) + x.shape[-1:])


def tree_gather(x, axis, size, bits):
    me = lax.axis_index(axis)
    held = []
    for bit in bits:
        other = lax.ppermute(x, axis, xor_pairs(size, bit))
        low = (me >> bit) & 1 == 0
        x = jnp.stack([jnp.where(low, x, other), jnp.where(low, other, x)], 0)
        held.insert(0, bit)
    count = len(bits)
    order = [held.index(bit) for bit in range(count - 1, -1, -1)]
    x = jnp.transpose(x, order + list(range(count, x.ndim)))
    return x.reshape((size * x.shape[count],) + x.shape[count + 1 :])


def exchange_sum(x, axis, size):
    spread = jnp.broadcast_to(x[None], (size,) + x.shape)
    return jnp.sum(lax.all_to_all(spread, axis, 0, 0, tiled=False), axis=0)


def exchange_scatter_sum(x, axis, size):
    blocks = x.reshape((size, x.shape[0] // size) + x.shape[1:])
    return jnp.sum(lax.all_to_all(blocks, axis, 0, 0, tiled=False), axis=0)


def exchange_gather(x, axis, size):
    spread = jnp.broadcast_to(x[None], (size,) + x.shape)
    out = lax.all_to_all(spread, axis, 0, 0, tiled=False)
    return out.reshape((size * x.shape[0],) + x.shape[1:])


def split_bf16(v):
    high = v.astype(jnp.bfloat16)
    return high, (v - high.astype(jnp.float32)).astype(jnp.bfloat16)


def split_products(x, gain, bias, weight):
    rows = x.shape[0]
    scaled_high, scaled_low = split_bf16(x * gain)
    gain_high, gain_low = split_bf16(gain[None])
    bias_high, bias_low = split_bf16(bias[None])
    lhs = jnp.concatenate([scaled_high, scaled_low, gain_high, gain_low, bias_high, bias_low])
    prod = jnp.dot(lhs, weight, preferred_element_type=jnp.float32)
    main = prod[:rows] + prod[rows : 2 * rows]
    base = 2 * rows
    terms = jnp.stack(
        [prod[base] + prod[base + 1], prod[base + 2] + prod[base + 3]]
    )
    return main, terms


def bit_order(size, first):
    bits = [b for b in first if (1 << b) < size]
    return bits + [b for b in range(size.bit_length() - 1) if b not in bits]


def on_device(
    hidden_in,
    norm1_gain,
    norm1_bias,
    norm2_gain,
    norm2_bias,
    w_qkv,
    b_qkv,
    w_out,
    b_out,
    w_up,
    b_up,
    w_down,
    b_down,
    key_cache,
    value_cache,
    lengths,
    assignment,
    gx_size,
    gy_size,
):
    requests = hidden_in.shape[0]
    rows_dev = key_cache.shape[0]
    heads_dev = key_cache.shape[1]
    gx_bits = bit_order(gx_size, (0, 2, 1, 3, 4))
    gy_bits = bit_order(gy_size, (0, 1, 2))
    wide_in = hidden_in.astype(jnp.float32)
    slot_ids = lax.iota(jnp.int32, requests)
    matches = assignment[:, None] == slot_ids[None, :]
    to_request = matches.astype(jnp.float32)
    to_slot = matches.T.astype(jnp.bfloat16)
    x_slot = jnp.dot(to_slot, hidden_in, preferred_element_type=jnp.float32)
    slot_len = jnp.sum(jnp.where(matches, lengths[:, None], 0), axis=0)
    my_len = lax.dynamic_slice_in_dim(slot_len, lax.axis_index("gx") * rows_dev, rows_dev, 0)
    qkv_cols = w_qkv.shape[1]
    up_cols = w_up.shape[1]
    gx_rows, gx_terms = split_products(x_slot, norm1_gain, norm1_bias, w_qkv)
    up_rows, up_terms = split_products(x_slot, norm2_gain, norm2_bias, w_up)
    local_stats = jnp.stack([jnp.sum(x_slot, axis=1), jnp.sum(x_slot * x_slot, axis=1)], axis=1)
    reduced = exchange_scatter_sum(
        jnp.concatenate([gx_rows, up_rows, local_stats], axis=1), "gx", gx_size
    )
    terms = tree_sum(jnp.concatenate([gx_terms, up_terms], axis=1), "gx", gx_size, gx_bits)
    row_mean = reduced[:, -2] / D
    row_var = reduced[:, -1] / D - row_mean * row_mean
    row_scale = lax.rsqrt(row_var + 1e-05)[:, None]
    row_mean = row_mean[:, None]
    qkv = (
        row_scale * (reduced[:, :qkv_cols] - row_mean * terms[0:1, :qkv_cols])
        + terms[1:2, :qkv_cols]
        + b_qkv
    )
    up = (
        row_scale
        * (reduced[:, qkv_cols : qkv_cols + up_cols] - row_mean * terms[0:1, qkv_cols:])
        + terms[1:2, qkv_cols:]
        + b_up
    )
    qkv = qkv.reshape(rows_dev, heads_dev, 3, HD)
    position = my_len - 1
    query = rotate(qkv[:, :, 0], position).astype(jnp.bfloat16)
    new_key = rotate(qkv[:, :, 1], position).astype(jnp.bfloat16)
    new_value = qkv[:, :, 2].astype(jnp.bfloat16)
    new_keys = key_cache
    new_values = value_cache
    zero_index = jnp.int32(0)
    for local_slot in range(rows_dev):
        slot_index = jnp.int32(local_slot)
        new_keys = lax.dynamic_update_slice(
            new_keys,
            new_key[local_slot][None, :, None, :],
            (slot_index, zero_index, position[local_slot], zero_index),
        )
        new_values = lax.dynamic_update_slice(
            new_values,
            new_value[local_slot][None, :, None, :],
            (slot_index, zero_index, position[local_slot], zero_index),
        )
    scores, valid = block_scores(query, new_keys, my_len)
    top_score = jnp.max(scores, axis=2)
    weights = jnp.where(valid, jnp.exp(scores - top_score[:, :, None]), 0.0)
    total = jnp.sum(weights, axis=2)
    weights_low = weights.astype(jnp.bfloat16)
    weighted = jnp.einsum(
        "shp,shpd->shd", weights_low, new_values, preferred_element_type=jnp.float32
    )
    attended = (weighted / total[:, :, None]).astype(jnp.bfloat16).reshape(rows_dev, heads_dev * HD)
    hidden = jax.nn.gelu(up, approximate=False).astype(jnp.bfloat16)
    gathered = exchange_gather(jnp.concatenate([attended, hidden], axis=1), "gx", gx_size)
    attn_cols = attended.shape[1]
    slot_part = jnp.dot(
        gathered[:, :attn_cols], w_out, preferred_element_type=jnp.float32
    ) + jnp.dot(gathered[:, attn_cols:], w_down, preferred_element_type=jnp.float32)
    branches = tree_sum(slot_part, "gy", gy_size, gy_bits)
    branches = jnp.dot(to_request, branches, precision=lax.Precision.HIGHEST)
    hidden_out = (wide_in + branches + b_out + b_down).astype(jnp.bfloat16)
    return (hidden_out, new_keys, new_values)


def solution(mesh):
    body = functools.partial(on_device, gx_size=mesh.shape["gx"], gy_size=mesh.shape["gy"])
    return jax.shard_map(
        body,
        mesh=mesh,
        in_specs=(
            P(None, "gx"),
            P("gx"),
            P("gx"),
            P("gx"),
            P("gx"),
            P("gx", "gy"),
            P("gy"),
            P("gy", "gx"),
            P("gx"),
            P("gx", "gy"),
            P("gy"),
            P("gy", "gx"),
            P("gx"),
            P("gx", "gy", None, None),
            P("gx", "gy", None, None),
            P(),
            P(),
        ),
        out_specs=(P(None, "gx"), P("gx", "gy", None, None), P("gx", "gy", None, None)),
        check_vma=False,
    )
```

```python
import functools

import jax
import jax.numpy as jnp
from jax import lax
from jax.sharding import PartitionSpec as P


D = 5120
HD = 128
ROT = 32


def rotate(tensor, position):
    half_rot = ROT // 2
    frequency = 10000.0 ** (-2.0 * jnp.arange(half_rot, dtype=jnp.float32) / ROT)
    angle = position.astype(jnp.float32)[:, None, None] * frequency
    cosine = jnp.cos(angle)
    sine = jnp.sin(angle)
    first_half = tensor[..., :half_rot]
    second_half = tensor[..., half_rot:ROT]
    return jnp.concatenate(
        [
            first_half * cosine - second_half * sine,
            second_half * cosine + first_half * sine,
            tensor[..., ROT:],
        ],
        axis=-1,
    )


def block_scores(query, keys, my_len):
    span_len = keys.shape[2]
    scores = jnp.einsum("shd,shpd->shp", query, keys, preferred_element_type=jnp.float32) * HD ** (
        -0.5
    )
    places = lax.iota(jnp.int32, span_len)
    valid = places[None, None, :] < my_len[:, None, None]
    return (jnp.where(valid, scores, -1e30), valid)


def xor_pairs(size, bit):
    return [(i, i ^ (1 << bit)) for i in range(size)]


def tree_sum(x, axis, size, bits):
    for bit in bits:
        x = x + lax.ppermute(x, axis, xor_pairs(size, bit))
    return x


def exchange_sum(x, axis, size):
    spread = jnp.broadcast_to(x[None], (size,) + x.shape)
    return jnp.sum(lax.all_to_all(spread, axis, 0, 0, tiled=False), axis=0)


def bit_order(size, first):
    bits = [b for b in first if (1 << b) < size]
    return bits + [b for b in range(size.bit_length() - 1) if b not in bits]


def layer(
    hidden_in,
    norm1_gain,
    norm1_bias,
    norm2_gain,
    norm2_bias,
    w_qkv,
    b_qkv,
    w_out,
    b_out,
    w_up,
    b_up,
    w_down,
    b_down,
    key_cache,
    value_cache,
    lengths,
    assignment,
    gx_size,
    gy_size,
):
    requests = hidden_in.shape[0]
    rows_dev = key_cache.shape[0]
    heads_dev = key_cache.shape[1]
    gy_bits = bit_order(gy_size, (0, 1, 2))
    wide_in = hidden_in.astype(jnp.float32)
    stats = exchange_sum(
        jnp.stack([jnp.sum(wide_in, axis=1), jnp.sum(wide_in * wide_in, axis=1)]),
        "gx",
        gx_size,
    )
    sum_rows, sum_squares = stats[0], stats[1]
    row_mean = sum_rows / D
    row_var = sum_squares / D - row_mean * row_mean
    normed = (wide_in - row_mean[:, None]) * lax.rsqrt(row_var + 1e-05)[:, None]
    attn_in = (normed * norm1_gain + norm1_bias).astype(jnp.bfloat16)
    mlp_in = (normed * norm2_gain + norm2_bias).astype(jnp.bfloat16)
    slot_ids = lax.iota(jnp.int32, requests)
    matches = assignment[:, None] == slot_ids[None, :]
    to_request = matches.astype(jnp.float32)
    to_slot = matches.T.astype(jnp.bfloat16)
    attn_slot = jnp.dot(to_slot, attn_in, preferred_element_type=jnp.float32).astype(jnp.bfloat16)
    mlp_slot = jnp.dot(to_slot, mlp_in, preferred_element_type=jnp.float32).astype(jnp.bfloat16)
    slot_len = jnp.sum(jnp.where(matches, lengths[:, None], 0), axis=0)
    my_len = lax.dynamic_slice_in_dim(slot_len, lax.axis_index("gx") * rows_dev, rows_dev, 0)
    qkv_cols = w_qkv.shape[1]
    blocks = (gx_size, requests // gx_size, attn_slot.shape[1])
    partial = jnp.concatenate(
        [
            jnp.einsum(
                "sbk,kn->sbn", attn_slot.reshape(blocks), w_qkv, preferred_element_type=jnp.float32
            ),
            jnp.einsum(
                "sbk,kn->sbn", mlp_slot.reshape(blocks), w_up, preferred_element_type=jnp.float32
            ),
        ],
        axis=2,
    )
    reduced = jnp.sum(lax.all_to_all(partial, "gx", 0, 0, tiled=False), axis=0)
    qkv = reduced[:, :qkv_cols] + b_qkv
    up = reduced[:, qkv_cols:] + b_up
    qkv = qkv.reshape(rows_dev, heads_dev, 3, HD)
    position = my_len - 1
    query = rotate(qkv[:, :, 0], position).astype(jnp.bfloat16)
    new_key = rotate(qkv[:, :, 1], position).astype(jnp.bfloat16)
    new_value = qkv[:, :, 2].astype(jnp.bfloat16)
    new_keys = jnp.where(slot_len[0] > 0, key_cache, jnp.zeros_like(key_cache))
    new_values = value_cache
    zero_index = jnp.int32(0)
    for local_slot in range(rows_dev):
        slot_index = jnp.int32(local_slot)
        new_keys = lax.dynamic_update_slice(
            new_keys,
            new_key[local_slot][None, :, None, :],
            (slot_index, zero_index, position[local_slot], zero_index),
        )
        new_values = lax.dynamic_update_slice(
            new_values,
            new_value[local_slot][None, :, None, :],
            (slot_index, zero_index, position[local_slot], zero_index),
        )
    scores, valid = block_scores(query, new_keys, my_len)
    top_score = jnp.max(scores, axis=2)
    weights = jnp.where(valid, jnp.exp(scores - top_score[:, :, None]), 0.0)
    total = jnp.sum(weights, axis=2)
    weights_low = weights.astype(jnp.bfloat16)
    weighted = jnp.einsum(
        "shp,shpd->shd", weights_low, new_values, preferred_element_type=jnp.float32
    )
    attended = (weighted / total[:, :, None]).astype(jnp.bfloat16).reshape(rows_dev, heads_dev * HD)
    hidden = jax.nn.gelu(up, approximate=False).astype(jnp.bfloat16)
    both = jnp.concatenate([attended, hidden], axis=1)
    gathered = lax.all_to_all(
        jnp.broadcast_to(both[None], (gx_size,) + both.shape), "gx", 0, 0, tiled=False
    )
    attn_cols = attended.shape[1]
    slot_part = (
        jnp.einsum(
            "sbk,kn->sbn", gathered[:, :, :attn_cols], w_out, preferred_element_type=jnp.float32
        )
        + jnp.einsum(
            "sbk,kn->sbn", gathered[:, :, attn_cols:], w_down, preferred_element_type=jnp.float32
        )
    ).reshape(requests, w_out.shape[1])
    branches = tree_sum(slot_part, "gy", gy_size, gy_bits)
    branches = jnp.dot(to_request, branches, precision=lax.Precision.HIGHEST)
    hidden_out = (wide_in + branches + b_out + b_down).astype(jnp.bfloat16)
    return (hidden_out, new_keys, new_values)


def solution(mesh):
    body = functools.partial(layer, gx_size=mesh.shape["gx"], gy_size=mesh.shape["gy"])
    return jax.shard_map(
        body,
        mesh=mesh,
        in_specs=(
            P(None, "gx"),
            P("gx"),
            P("gx"),
            P("gx"),
            P("gx"),
            P("gx", "gy"),
            P("gy"),
            P("gy", "gx"),
            P("gx"),
            P("gx", "gy"),
            P("gy"),
            P("gy", "gx"),
            P("gx"),
            P("gx", "gy", None, None),
            P("gx", "gy", None, None),
            P(),
            P(),
        ),
        out_specs=(P(None, "gx"), P("gx", "gy", None, None), P("gx", "gy", None, None)),
        check_vma=False,
    )
```

```python
import functools

import jax
import jax.numpy as jnp
from jax import lax
from jax.sharding import PartitionSpec as P


D = 5120
HD = 128
ROT = 32


def rotate(tensor, position):
    half_rot = ROT // 2
    frequency = 10000.0 ** (-2.0 * jnp.arange(half_rot, dtype=jnp.float32) / ROT)
    angle = position.astype(jnp.float32)[:, None, None] * frequency
    cosine = jnp.cos(angle)
    sine = jnp.sin(angle)
    first_half = tensor[..., :half_rot]
    second_half = tensor[..., half_rot:ROT]
    return jnp.concatenate(
        [
            first_half * cosine - second_half * sine,
            second_half * cosine + first_half * sine,
            tensor[..., ROT:],
        ],
        axis=-1,
    )


def block_scores(query, keys, my_len):
    span_len = keys.shape[2]
    scores = jnp.einsum("shd,shpd->shp", query, keys, preferred_element_type=jnp.float32) * HD ** (
        -0.5
    )
    places = lax.iota(jnp.int32, span_len)
    valid = places[None, None, :] < my_len[:, None, None]
    return (jnp.where(valid, scores, -1e30), valid)


def xor_pairs(size, bit):
    return [(i, i ^ (1 << bit)) for i in range(size)]


def exchange_sum(x, axis, size):
    spread = jnp.broadcast_to(x[None], (size,) + x.shape)
    return jnp.sum(lax.all_to_all(spread, axis, 0, 0, tiled=False), axis=0)


def pair_sum(x, axis, rounds):
    for pairs in rounds:
        x = x + lax.ppermute(x, axis, pairs)
    return x


def gy_pairs(size):
    rounds = [xor_pairs(size, bit) for bit in range(size.bit_length() - 1)]
    if size == 8:
        rounds[2] = [(i, (3 - i // 2) * 2 + i % 2) for i in range(size)]
    return rounds


def layer(
    hidden_in,
    norm1_gain,
    norm1_bias,
    norm2_gain,
    norm2_bias,
    w_qkv,
    b_qkv,
    w_out,
    b_out,
    w_up,
    b_up,
    w_down,
    b_down,
    key_cache,
    value_cache,
    lengths,
    assignment,
    gx_size,
    gy_size,
):
    requests = hidden_in.shape[0]
    rows_dev = key_cache.shape[0]
    heads_dev = key_cache.shape[1]
    wide_in = hidden_in.astype(jnp.float32)
    stats = exchange_sum(
        jnp.stack([jnp.sum(wide_in, axis=1), jnp.sum(wide_in * wide_in, axis=1)]),
        "gx",
        gx_size,
    )
    sum_rows, sum_squares = stats[0], stats[1]
    row_mean = sum_rows / D
    row_var = sum_squares / D - row_mean * row_mean
    normed = (wide_in - row_mean[:, None]) * lax.rsqrt(row_var + 1e-05)[:, None]
    attn_in = (normed * norm1_gain + norm1_bias).astype(jnp.bfloat16)
    mlp_in = (normed * norm2_gain + norm2_bias).astype(jnp.bfloat16)
    slot_ids = lax.iota(jnp.int32, requests)
    matches = assignment[:, None] == slot_ids[None, :]
    to_request = matches.astype(jnp.float32)
    to_slot = matches.T.astype(jnp.bfloat16)
    attn_slot = jnp.dot(to_slot, attn_in, preferred_element_type=jnp.float32).astype(jnp.bfloat16)
    mlp_slot = jnp.dot(to_slot, mlp_in, preferred_element_type=jnp.float32).astype(jnp.bfloat16)
    slot_len = jnp.sum(jnp.where(matches, lengths[:, None], 0), axis=0)
    my_len = lax.dynamic_slice_in_dim(slot_len, lax.axis_index("gx") * rows_dev, rows_dev, 0)
    qkv_cols = w_qkv.shape[1]
    blocks = (gx_size, requests // gx_size, attn_slot.shape[1])
    partial = jnp.concatenate(
        [
            jnp.einsum(
                "sbk,kn->sbn", attn_slot.reshape(blocks), w_qkv, preferred_element_type=jnp.float32
            ),
            jnp.einsum(
                "sbk,kn->sbn", mlp_slot.reshape(blocks), w_up, preferred_element_type=jnp.float32
            ),
        ],
        axis=2,
    )
    reduced = jnp.sum(lax.all_to_all(partial, "gx", 0, 0, tiled=False), axis=0)
    qkv = reduced[:, :qkv_cols] + b_qkv
    up = reduced[:, qkv_cols:] + b_up
    qkv = qkv.reshape(rows_dev, heads_dev, 3, HD)
    position = my_len - 1
    query = rotate(qkv[:, :, 0], position).astype(jnp.bfloat16)
    new_key = rotate(qkv[:, :, 1], position).astype(jnp.bfloat16)
    new_value = qkv[:, :, 2].astype(jnp.bfloat16)
    new_keys = jnp.where(slot_len[0] > 0, key_cache, jnp.zeros_like(key_cache))
    new_values = jnp.where(slot_len[0] > 0, value_cache, jnp.zeros_like(value_cache))
    zero_index = jnp.int32(0)
    for local_slot in range(rows_dev):
        slot_index = jnp.int32(local_slot)
        new_keys = lax.dynamic_update_slice(
            new_keys,
            new_key[local_slot][None, :, None, :],
            (slot_index, zero_index, position[local_slot], zero_index),
        )
        new_values = lax.dynamic_update_slice(
            new_values,
            new_value[local_slot][None, :, None, :],
            (slot_index, zero_index, position[local_slot], zero_index),
        )
    old_scores, valid = block_scores(query, key_cache, my_len)
    fresh = jnp.einsum(
        "shd,shd->sh", query, new_key, preferred_element_type=jnp.float32
    ) * HD ** (-0.5)
    places = lax.iota(jnp.int32, key_cache.shape[2])
    scores = jnp.where(
        places[None, None, :] == position[:, None, None], fresh[:, :, None], old_scores
    )
    top_score = jnp.max(scores, axis=2)
    weights = jnp.where(valid, jnp.exp(scores - top_score[:, :, None]), 0.0)
    total = jnp.sum(weights, axis=2)
    weights_low = weights.astype(jnp.bfloat16)
    at_new = places[None, None, :] == position[:, None, None]
    weighted = jnp.einsum(
        "shp,shpd->shd",
        jnp.where(at_new, jnp.zeros_like(weights_low), weights_low),
        value_cache,
        preferred_element_type=jnp.float32,
    ) + jnp.sum(
        jnp.where(at_new, weights_low, jnp.zeros_like(weights_low)).astype(jnp.float32), axis=2
    )[:, :, None] * new_value.astype(jnp.float32)
    attended = (weighted / total[:, :, None]).astype(jnp.bfloat16).reshape(rows_dev, heads_dev * HD)
    hidden = jax.nn.gelu(up, approximate=False).astype(jnp.bfloat16)
    both = jnp.concatenate([attended, hidden], axis=1)
    gathered = lax.all_to_all(
        jnp.broadcast_to(both[None], (gx_size,) + both.shape), "gx", 0, 0, tiled=False
    )
    attn_cols = attended.shape[1]
    slot_part = (
        jnp.einsum(
            "sbk,kn->sbn", gathered[:, :, :attn_cols], w_out, preferred_element_type=jnp.float32
        )
        + jnp.einsum(
            "sbk,kn->sbn", gathered[:, :, attn_cols:], w_down, preferred_element_type=jnp.float32
        )
    ).reshape(requests, w_out.shape[1])
    branches = pair_sum(slot_part, "gy", gy_pairs(gy_size))
    branches = jnp.dot(to_request, branches, precision=lax.Precision.HIGHEST)
    hidden_out = (wide_in + branches + b_out + b_down).astype(jnp.bfloat16)
    return (hidden_out, new_keys, new_values)


def solution(mesh):
    body = functools.partial(layer, gx_size=mesh.shape["gx"], gy_size=mesh.shape["gy"])
    return jax.shard_map(
        body,
        mesh=mesh,
        in_specs=(
            P(None, "gx"),
            P("gx"),
            P("gx"),
            P("gx"),
            P("gx"),
            P("gx", "gy"),
            P("gy"),
            P("gy", "gx"),
            P("gx"),
            P("gx", "gy"),
            P("gy"),
            P("gy", "gx"),
            P("gx"),
            P("gx", "gy", None, None),
            P("gx", "gy", None, None),
            P(),
            P(),
        ),
        out_specs=(P(None, "gx"), P("gx", "gy", None, None), P("gx", "gy", None, None)),
        check_vma=False,
    )
```

```python
import functools

import jax
import jax.numpy as jnp
from jax import lax
from jax.sharding import PartitionSpec as P


D = 5120
HD = 128
ROT = 32


def rotate(tensor, position):
    half_rot = ROT // 2
    frequency = 10000.0 ** (-2.0 * jnp.arange(half_rot, dtype=jnp.float32) / ROT)
    angle = position.astype(jnp.float32)[:, None, None] * frequency
    cosine = jnp.cos(angle)
    sine = jnp.sin(angle)
    first_half = tensor[..., :half_rot]
    second_half = tensor[..., half_rot:ROT]
    return jnp.concatenate(
        [
            first_half * cosine - second_half * sine,
            second_half * cosine + first_half * sine,
            tensor[..., ROT:],
        ],
        axis=-1,
    )


def block_scores(query, keys, my_len):
    span_len = keys.shape[2]
    scores = jnp.einsum("shd,shpd->shp", query, keys, preferred_element_type=jnp.float32) * HD ** (
        -0.5
    )
    places = lax.iota(jnp.int32, span_len)
    valid = places[None, None, :] < my_len[:, None, None]
    return (jnp.where(valid, scores, -1e30), valid)


def xor_pairs(size, bit):
    return [(i, i ^ (1 << bit)) for i in range(size)]


def exchange_sum(x, axis, size):
    spread = jnp.broadcast_to(x[None], (size,) + x.shape)
    return jnp.sum(lax.all_to_all(spread, axis, 0, 0, tiled=False), axis=0)


def pair_sum(x, axis, rounds):
    for pairs in rounds:
        x = x + lax.ppermute(x, axis, pairs)
    return x


def gy_pairs(size):
    rounds = [xor_pairs(size, bit) for bit in range(size.bit_length() - 1)]
    if size == 8:
        rounds[2] = [(i, (3 - i // 2) * 2 + i % 2) for i in range(size)]
    return rounds


def layer(
    hidden_in,
    norm1_gain,
    norm1_bias,
    norm2_gain,
    norm2_bias,
    w_qkv,
    b_qkv,
    w_out,
    b_out,
    w_up,
    b_up,
    w_down,
    b_down,
    key_cache,
    value_cache,
    lengths,
    assignment,
    gx_size,
    gy_size,
):
    requests = hidden_in.shape[0]
    rows_dev = key_cache.shape[0]
    heads_dev = key_cache.shape[1]
    wide_in = hidden_in.astype(jnp.float32)
    stats = exchange_sum(
        jnp.stack([jnp.sum(wide_in, axis=1), jnp.sum(wide_in * wide_in, axis=1)]),
        "gx",
        gx_size,
    )
    sum_rows, sum_squares = stats[0], stats[1]
    row_mean = sum_rows / D
    row_var = sum_squares / D - row_mean * row_mean
    normed = (wide_in - row_mean[:, None]) * lax.rsqrt(row_var + 1e-05)[:, None]
    attn_in = (normed * norm1_gain + norm1_bias).astype(jnp.bfloat16)
    mlp_in = (normed * norm2_gain + norm2_bias).astype(jnp.bfloat16)
    slot_ids = lax.iota(jnp.int32, requests)
    matches = assignment[:, None] == slot_ids[None, :]
    to_request = matches.astype(jnp.float32)
    to_slot = matches.T.astype(jnp.bfloat16)
    attn_slot = jnp.dot(to_slot, attn_in, preferred_element_type=jnp.float32).astype(jnp.bfloat16)
    mlp_slot = jnp.dot(to_slot, mlp_in, preferred_element_type=jnp.float32).astype(jnp.bfloat16)
    slot_len = jnp.sum(jnp.where(matches, lengths[:, None], 0), axis=0)
    my_len = lax.dynamic_slice_in_dim(slot_len, lax.axis_index("gx") * rows_dev, rows_dev, 0)
    qkv_cols = w_qkv.shape[1]
    blocks = (gx_size, requests // gx_size, attn_slot.shape[1])
    partial = jnp.concatenate(
        [
            jnp.einsum(
                "sbk,kn->sbn", attn_slot.reshape(blocks), w_qkv, preferred_element_type=jnp.float32
            ),
            jnp.einsum(
                "sbk,kn->sbn", mlp_slot.reshape(blocks), w_up, preferred_element_type=jnp.float32
            ),
        ],
        axis=2,
    )
    reduced = jnp.sum(lax.all_to_all(partial, "gx", 0, 0, tiled=False), axis=0)
    qkv = reduced[:, :qkv_cols] + b_qkv
    up = reduced[:, qkv_cols:] + b_up
    qkv = qkv.reshape(rows_dev, heads_dev, 3, HD)
    position = my_len - 1
    query = rotate(qkv[:, :, 0], position).astype(jnp.bfloat16)
    new_key = rotate(qkv[:, :, 1], position).astype(jnp.bfloat16)
    new_value = qkv[:, :, 2].astype(jnp.bfloat16)
    old_scores, valid = block_scores(query, key_cache, my_len)
    fresh = jnp.einsum(
        "shd,shd->sh", query, new_key, preferred_element_type=jnp.float32
    ) * HD ** (-0.5)
    places = lax.iota(jnp.int32, key_cache.shape[2])
    scores = jnp.where(
        places[None, None, :] == position[:, None, None], fresh[:, :, None], old_scores
    )
    top_score = jnp.max(scores, axis=2)
    weights = jnp.where(valid, jnp.exp(scores - top_score[:, :, None]), 0.0)
    total = jnp.sum(weights, axis=2)
    weights_low = weights.astype(jnp.bfloat16)
    at_new = places[None, None, :] == position[:, None, None]
    weighted = jnp.einsum(
        "shp,shpd->shd",
        jnp.where(at_new, jnp.zeros_like(weights_low), weights_low),
        value_cache,
        preferred_element_type=jnp.float32,
    ) + jnp.sum(
        jnp.where(at_new, weights_low, jnp.zeros_like(weights_low)).astype(jnp.float32), axis=2
    )[:, :, None] * new_value.astype(jnp.float32)
    attended = (weighted / total[:, :, None]).astype(jnp.bfloat16).reshape(rows_dev, heads_dev * HD)
    hidden = jax.nn.gelu(up, approximate=False).astype(jnp.bfloat16)
    at_row = (places[None, :] == position[:, None])[:, None, :, None]
    new_keys = jnp.where(at_row, new_key[:, :, None, :], key_cache)
    new_values = jnp.where(at_row, new_value[:, :, None, :], value_cache)
    both = jnp.concatenate([attended, hidden], axis=1)
    gathered = lax.all_to_all(
        jnp.broadcast_to(both[None], (gx_size,) + both.shape), "gx", 0, 0, tiled=False
    )
    attn_cols = attended.shape[1]
    slot_part = (
        jnp.einsum(
            "sbk,kn->sbn", gathered[:, :, :attn_cols], w_out, preferred_element_type=jnp.float32
        )
        + jnp.einsum(
            "sbk,kn->sbn", gathered[:, :, attn_cols:], w_down, preferred_element_type=jnp.float32
        )
    ).reshape(requests, w_out.shape[1])
    branches = pair_sum(slot_part, "gy", gy_pairs(gy_size))
    branches = jnp.dot(to_request, branches, precision=lax.Precision.HIGHEST)
    hidden_out = (wide_in + branches + b_out + b_down).astype(jnp.bfloat16)
    return (hidden_out, new_keys, new_values)


def solution(mesh):
    body = functools.partial(layer, gx_size=mesh.shape["gx"], gy_size=mesh.shape["gy"])
    return jax.shard_map(
        body,
        mesh=mesh,
        in_specs=(
            P(None, "gx"),
            P("gx"),
            P("gx"),
            P("gx"),
            P("gx"),
            P("gx", "gy"),
            P("gy"),
            P("gy", "gx"),
            P("gx"),
            P("gx", "gy"),
            P("gy"),
            P("gy", "gx"),
            P("gx"),
            P("gx", "gy", None, None),
            P("gx", "gy", None, None),
            P(),
            P(),
        ),
        out_specs=(P(None, "gx"), P("gx", "gy", None, None), P("gx", "gy", None, None)),
        check_vma=False,
    )
```

```python
import functools

import jax
import jax.numpy as jnp
from jax import lax
from jax.sharding import PartitionSpec as P


D = 5120
HD = 128
ROT = 32


def rotate(tensor, position):
    half_rot = ROT // 2
    frequency = 10000.0 ** (-2.0 * jnp.arange(half_rot, dtype=jnp.float32) / ROT)
    angle = position.astype(jnp.float32)[:, None, None] * frequency
    cosine = jnp.cos(angle)
    sine = jnp.sin(angle)
    first_half = tensor[..., :half_rot]
    second_half = tensor[..., half_rot:ROT]
    return jnp.concatenate(
        [
            first_half * cosine - second_half * sine,
            second_half * cosine + first_half * sine,
            tensor[..., ROT:],
        ],
        axis=-1,
    )


def block_scores(query, keys, my_len):
    span_len = keys.shape[2]
    scores = jnp.einsum("shd,shpd->shp", query, keys, preferred_element_type=jnp.float32) * HD ** (
        -0.5
    )
    places = lax.iota(jnp.int32, span_len)
    valid = places[None, None, :] < my_len[:, None, None]
    return (jnp.where(valid, scores, -1e30), valid)


def xor_pairs(size, bit):
    return [(i, i ^ (1 << bit)) for i in range(size)]


def exchange_sum(x, axis, size):
    spread = jnp.broadcast_to(x[None], (size,) + x.shape)
    return jnp.sum(lax.all_to_all(spread, axis, 0, 0, tiled=False), axis=0)


def pair_sum(x, axis, rounds):
    for pairs in rounds:
        x = x + lax.ppermute(x, axis, pairs)
    return x


def gy_pairs(size):
    rounds = [xor_pairs(size, bit) for bit in range(size.bit_length() - 1)]
    if size == 8:
        rounds[2] = [(i, (3 - i // 2) * 2 + i % 2) for i in range(size)]
    return rounds


def layer(
    hidden_in,
    norm1_gain,
    norm1_bias,
    norm2_gain,
    norm2_bias,
    w_qkv,
    b_qkv,
    w_out,
    b_out,
    w_up,
    b_up,
    w_down,
    b_down,
    key_cache,
    value_cache,
    lengths,
    assignment,
    gx_size,
    gy_size,
):
    requests = hidden_in.shape[0]
    rows_dev = key_cache.shape[0]
    heads_dev = key_cache.shape[1]
    wide_in = hidden_in.astype(jnp.float32)
    stats = exchange_sum(
        jnp.stack([jnp.sum(wide_in, axis=1), jnp.sum(wide_in * wide_in, axis=1)]),
        "gx",
        gx_size,
    )
    slot_ids = lax.iota(jnp.int32, requests)
    matches = assignment[:, None] == slot_ids[None, :]
    to_request = matches.astype(jnp.float32)
    x_slot = jnp.dot(matches.T.astype(jnp.bfloat16), hidden_in, preferred_element_type=jnp.float32)
    w_both = jnp.concatenate([w_out, w_down], axis=0)
    stats = jnp.sum(jnp.where(matches[None], stats[:, :, None], 0.0), axis=1)
    sum_rows, sum_squares = stats[0], stats[1]
    row_mean = sum_rows / D
    row_var = sum_squares / D - row_mean * row_mean
    normed = (x_slot - row_mean[:, None]) * lax.rsqrt(row_var + 1e-05)[:, None]
    attn_slot = (normed * norm1_gain + norm1_bias).astype(jnp.bfloat16)
    mlp_slot = (normed * norm2_gain + norm2_bias).astype(jnp.bfloat16)
    slot_len = jnp.sum(jnp.where(matches, lengths[:, None], 0), axis=0)
    my_len = lax.dynamic_slice_in_dim(slot_len, lax.axis_index("gx") * rows_dev, rows_dev, 0)
    qkv_cols = w_qkv.shape[1]
    blocks = (gx_size, requests // gx_size, attn_slot.shape[1])
    partial = jnp.concatenate(
        [
            jnp.einsum(
                "sbk,kn->sbn", attn_slot.reshape(blocks), w_qkv, preferred_element_type=jnp.float32
            ),
            jnp.einsum(
                "sbk,kn->sbn", mlp_slot.reshape(blocks), w_up, preferred_element_type=jnp.float32
            ),
        ],
        axis=2,
    )
    reduced = jnp.sum(lax.all_to_all(partial, "gx", 0, 0, tiled=False), axis=0)
    qkv = reduced[:, :qkv_cols] + b_qkv
    up = reduced[:, qkv_cols:] + b_up
    qkv = qkv.reshape(rows_dev, heads_dev, 3, HD)
    position = my_len - 1
    query = rotate(qkv[:, :, 0], position).astype(jnp.bfloat16)
    new_key = rotate(qkv[:, :, 1], position).astype(jnp.bfloat16)
    new_value = qkv[:, :, 2].astype(jnp.bfloat16)
    old_scores, valid = block_scores(query, key_cache, my_len)
    fresh = jnp.einsum(
        "shd,shd->sh", query, new_key, preferred_element_type=jnp.float32
    ) * HD ** (-0.5)
    places = lax.iota(jnp.int32, key_cache.shape[2])
    scores = jnp.where(
        places[None, None, :] == position[:, None, None], fresh[:, :, None], old_scores
    )
    top_score = jnp.max(scores, axis=2)
    weights = jnp.where(valid, jnp.exp(scores - top_score[:, :, None]), 0.0)
    total = jnp.sum(weights, axis=2)
    weights_low = weights.astype(jnp.bfloat16)
    at_new = places[None, None, :] == position[:, None, None]
    weighted = jnp.einsum(
        "shp,shpd->shd",
        jnp.where(at_new, jnp.zeros_like(weights_low), weights_low),
        value_cache,
        preferred_element_type=jnp.float32,
    ) + jnp.sum(
        jnp.where(at_new, weights_low, jnp.zeros_like(weights_low)).astype(jnp.float32), axis=2
    )[:, :, None] * new_value.astype(jnp.float32)
    attended = (weighted / total[:, :, None]).astype(jnp.bfloat16).reshape(rows_dev, heads_dev * HD)
    hidden = jax.nn.gelu(up, approximate=False).astype(jnp.bfloat16)
    at_row = (places[None, :] == position[:, None])[:, None, :, None]
    new_keys = jnp.where(at_row, new_key[:, :, None, :], key_cache)
    new_values = jnp.where(at_row, new_value[:, :, None, :], value_cache)
    both = jnp.concatenate([attended, hidden], axis=1)
    gathered = lax.all_to_all(
        jnp.broadcast_to(both[None], (gx_size,) + both.shape), "gx", 0, 0, tiled=False
    )
    slot_part = jnp.einsum(
        "sbk,kn->sbn", gathered, w_both, preferred_element_type=jnp.float32
    ).reshape(requests, w_out.shape[1])
    branches = pair_sum(slot_part, "gy", gy_pairs(gy_size))
    branches = jnp.dot(to_request, branches, precision=lax.Precision.HIGHEST)
    hidden_out = (wide_in + branches + b_out + b_down).astype(jnp.bfloat16)
    return (hidden_out, new_keys, new_values)


def solution(mesh):
    body = functools.partial(layer, gx_size=mesh.shape["gx"], gy_size=mesh.shape["gy"])
    return jax.shard_map(
        body,
        mesh=mesh,
        in_specs=(
            P(None, "gx"),
            P("gx"),
            P("gx"),
            P("gx"),
            P("gx"),
            P("gx", "gy"),
            P("gy"),
            P("gy", "gx"),
            P("gx"),
            P("gx", "gy"),
            P("gy"),
            P("gy", "gx"),
            P("gx"),
            P("gx", "gy", None, None),
            P("gx", "gy", None, None),
            P(),
            P(),
        ),
        out_specs=(P(None, "gx"), P("gx", "gy", None, None), P("gx", "gy", None, None)),
        check_vma=False,
    )
```

```python
import functools

import jax
import jax.numpy as jnp
from jax import lax
from jax.sharding import PartitionSpec as P


D = 5120
HD = 128
ROT = 32


def rotate(tensor, position):
    half_rot = ROT // 2
    frequency = 10000.0 ** (-2.0 * jnp.arange(half_rot, dtype=jnp.float32) / ROT)
    angle = position.astype(jnp.float32)[:, None, None] * frequency
    cosine = jnp.cos(angle)
    sine = jnp.sin(angle)
    first_half = tensor[..., :half_rot]
    second_half = tensor[..., half_rot:ROT]
    return jnp.concatenate(
        [
            first_half * cosine - second_half * sine,
            second_half * cosine + first_half * sine,
            tensor[..., ROT:],
        ],
        axis=-1,
    )


def block_scores(query, keys, my_len):
    span_len = keys.shape[2]
    scores = jnp.einsum("shd,shpd->shp", query, keys, preferred_element_type=jnp.float32) * HD ** (
        -0.5
    )
    places = lax.iota(jnp.int32, span_len)
    valid = places[None, None, :] < my_len[:, None, None]
    return (jnp.where(valid, scores, -1e30), valid)


def xor_pairs(size, bit):
    return [(i, i ^ (1 << bit)) for i in range(size)]


def exchange_sum(x, axis, size):
    spread = jnp.broadcast_to(x[None], (size,) + x.shape)
    return jnp.sum(lax.all_to_all(spread, axis, 0, 0, tiled=False), axis=0)


def pair_sum(x, axis, rounds):
    for pairs in rounds:
        x = x + lax.ppermute(x, axis, pairs)
    return x


def gy_pairs(size):
    rounds = [xor_pairs(size, bit) for bit in range(size.bit_length() - 1)]
    if size == 8:
        rounds[2] = [(i, (3 - i // 2) * 2 + i % 2) for i in range(size)]
    return rounds


def layer(
    hidden_in,
    norm1_gain,
    norm1_bias,
    norm2_gain,
    norm2_bias,
    w_qkv,
    b_qkv,
    w_out,
    b_out,
    w_up,
    b_up,
    w_down,
    b_down,
    key_cache,
    value_cache,
    lengths,
    assignment,
    gx_size,
    gy_size,
):
    requests = hidden_in.shape[0]
    rows_dev = key_cache.shape[0]
    heads_dev = key_cache.shape[1]
    wide_in = hidden_in.astype(jnp.float32)
    stats = exchange_sum(
        jnp.stack([jnp.sum(wide_in, axis=1), jnp.sum(wide_in * wide_in, axis=1)]),
        "gx",
        gx_size,
    )
    slot_ids = lax.iota(jnp.int32, requests)
    matches = assignment[:, None] == slot_ids[None, :]
    to_request = matches.astype(jnp.float32)
    x_slot = jnp.dot(matches.T.astype(jnp.bfloat16), hidden_in, preferred_element_type=jnp.float32)
    w_both = jnp.concatenate([w_out, w_down], axis=0)
    stats = jnp.sum(jnp.where(matches[None], stats[:, :, None], 0.0), axis=1)
    sum_rows, sum_squares = stats[0], stats[1]
    row_mean = sum_rows / D
    row_var = sum_squares / D - row_mean * row_mean
    normed = (x_slot - row_mean[:, None]) * lax.rsqrt(row_var + 1e-05)[:, None]
    attn_slot = (normed * norm1_gain + norm1_bias).astype(jnp.bfloat16)
    mlp_slot = (normed * norm2_gain + norm2_bias).astype(jnp.bfloat16)
    slot_len = jnp.sum(jnp.where(matches, lengths[:, None], 0), axis=0)
    my_len = lax.dynamic_slice_in_dim(slot_len, lax.axis_index("gx") * rows_dev, rows_dev, 0)
    qkv_cols = w_qkv.shape[1]
    partial = jnp.concatenate(
        [
            jnp.dot(attn_slot, w_qkv, preferred_element_type=jnp.float32),
            jnp.dot(mlp_slot, w_up, preferred_element_type=jnp.float32),
        ],
        axis=1,
    )
    received = lax.all_to_all(partial, "gx", 0, 1, tiled=True)
    reduced = jnp.sum(received.reshape(rows_dev, gx_size, partial.shape[1]), axis=1)
    qkv = reduced[:, :qkv_cols] + b_qkv
    up = reduced[:, qkv_cols:] + b_up
    qkv = qkv.reshape(rows_dev, heads_dev, 3, HD)
    position = my_len - 1
    query = rotate(qkv[:, :, 0], position).astype(jnp.bfloat16)
    new_key = rotate(qkv[:, :, 1], position).astype(jnp.bfloat16)
    new_value = qkv[:, :, 2].astype(jnp.bfloat16)
    old_scores, valid = block_scores(query, key_cache, my_len)
    fresh = jnp.einsum(
        "shd,shd->sh", query, new_key, preferred_element_type=jnp.float32
    ) * HD ** (-0.5)
    places = lax.iota(jnp.int32, key_cache.shape[2])
    scores = jnp.where(
        places[None, None, :] == position[:, None, None], fresh[:, :, None], old_scores
    )
    top_score = jnp.max(scores, axis=2)
    weights = jnp.where(valid, jnp.exp(scores - top_score[:, :, None]), 0.0)
    total = jnp.sum(weights, axis=2)
    weights_low = weights.astype(jnp.bfloat16)
    at_new = places[None, None, :] == position[:, None, None]
    weighted = jnp.einsum(
        "shp,shpd->shd",
        jnp.where(at_new, jnp.zeros_like(weights_low), weights_low),
        value_cache,
        preferred_element_type=jnp.float32,
    ) + jnp.sum(
        jnp.where(at_new, weights_low, jnp.zeros_like(weights_low)).astype(jnp.float32), axis=2
    )[:, :, None] * new_value.astype(jnp.float32)
    attended = (weighted / total[:, :, None]).astype(jnp.bfloat16).reshape(rows_dev, heads_dev * HD)
    hidden = jax.nn.gelu(up, approximate=False).astype(jnp.bfloat16)
    at_row = (places[None, :] == position[:, None])[:, None, :, None]
    new_keys = jnp.where(at_row, new_key[:, :, None, :], key_cache)
    new_values = jnp.where(at_row, new_value[:, :, None, :], value_cache)
    both = jnp.concatenate([attended, hidden], axis=1)
    gathered = lax.all_to_all(
        jnp.broadcast_to(both[None], (gx_size,) + both.shape), "gx", 0, 0, tiled=False
    )
    slot_part = jnp.einsum(
        "sbk,kn->sbn", gathered, w_both, preferred_element_type=jnp.float32
    ).reshape(requests, w_out.shape[1])
    branches = pair_sum(slot_part, "gy", gy_pairs(gy_size))
    branches = jnp.dot(to_request, branches, precision=lax.Precision.HIGHEST)
    hidden_out = (wide_in + branches + b_out + b_down).astype(jnp.bfloat16)
    return (hidden_out, new_keys, new_values)


def solution(mesh):
    body = functools.partial(layer, gx_size=mesh.shape["gx"], gy_size=mesh.shape["gy"])
    return jax.shard_map(
        body,
        mesh=mesh,
        in_specs=(
            P(None, "gx"),
            P("gx"),
            P("gx"),
            P("gx"),
            P("gx"),
            P("gx", "gy"),
            P("gy"),
            P("gy", "gx"),
            P("gx"),
            P("gx", "gy"),
            P("gy"),
            P("gy", "gx"),
            P("gx"),
            P("gx", "gy", None, None),
            P("gx", "gy", None, None),
            P(),
            P(),
        ),
        out_specs=(P(None, "gx"), P("gx", "gy", None, None), P("gx", "gy", None, None)),
        check_vma=False,
    )
```

```python
import functools

import jax
import jax.numpy as jnp
from jax import lax
from jax.sharding import PartitionSpec as P


D = 5120
HD = 128
ROT = 32


def rotate(tensor, position):
    half_rot = ROT // 2
    frequency = 10000.0 ** (-2.0 * jnp.arange(half_rot, dtype=jnp.float32) / ROT)
    angle = position.astype(jnp.float32)[:, None, None] * frequency
    cosine = jnp.cos(angle)
    sine = jnp.sin(angle)
    first_half = tensor[..., :half_rot]
    second_half = tensor[..., half_rot:ROT]
    return jnp.concatenate(
        [
            first_half * cosine - second_half * sine,
            second_half * cosine + first_half * sine,
            tensor[..., ROT:],
        ],
        axis=-1,
    )


def block_scores(query, keys, my_len):
    span_len = keys.shape[2]
    scores = jnp.einsum("shd,shpd->shp", query, keys, preferred_element_type=jnp.float32) * HD ** (
        -0.5
    )
    places = lax.iota(jnp.int32, span_len)
    valid = places[None, None, :] < my_len[:, None, None]
    return (jnp.where(valid, scores, -1e30), valid)


def xor_pairs(size, bit):
    return [(i, i ^ (1 << bit)) for i in range(size)]


def exchange_sum(x, axis, size):
    spread = jnp.broadcast_to(x[None], (size,) + x.shape)
    return jnp.sum(lax.all_to_all(spread, axis, 0, 0, tiled=False), axis=0)


def pair_sum(x, axis, rounds):
    for pairs in rounds:
        x = x + lax.ppermute(x, axis, pairs)
    return x


def gy_pairs(size):
    rounds = [xor_pairs(size, bit) for bit in range(size.bit_length() - 1)]
    if size == 8:
        rounds[2] = [(i, (3 - i // 2) * 2 + i % 2) for i in range(size)]
    return rounds


def layer(
    hidden_in,
    norm1_gain,
    norm1_bias,
    norm2_gain,
    norm2_bias,
    w_qkv,
    b_qkv,
    w_out,
    b_out,
    w_up,
    b_up,
    w_down,
    b_down,
    key_cache,
    value_cache,
    lengths,
    assignment,
    gx_size,
    gy_size,
):
    requests = hidden_in.shape[0]
    rows_dev = key_cache.shape[0]
    heads_dev = key_cache.shape[1]
    wide_in = hidden_in.astype(jnp.float32)
    stats = exchange_sum(
        jnp.concatenate([jnp.sum(wide_in, axis=1), jnp.sum(wide_in * wide_in, axis=1)]),
        "gx",
        gx_size,
    ).reshape(2, requests)
    slot_ids = lax.iota(jnp.int32, requests)
    matches = assignment[:, None] == slot_ids[None, :]
    to_request = matches.astype(jnp.float32)
    x_slot = jnp.dot(matches.T.astype(jnp.bfloat16), hidden_in, preferred_element_type=jnp.float32)
    w_both = lax.optimization_barrier(jnp.concatenate([w_out, w_down], axis=0))
    stats = jnp.sum(jnp.where(matches[None], stats[:, :, None], 0.0), axis=1)
    sum_rows, sum_squares = stats[0], stats[1]
    row_mean = sum_rows / D
    row_var = sum_squares / D - row_mean * row_mean
    normed = (x_slot - row_mean[:, None]) * lax.rsqrt(row_var + 1e-05)[:, None]
    attn_slot = (normed * norm1_gain + norm1_bias).astype(jnp.bfloat16)
    mlp_slot = (normed * norm2_gain + norm2_bias).astype(jnp.bfloat16)
    slot_len = jnp.sum(jnp.where(matches, lengths[:, None], 0), axis=0)
    my_len = lax.dynamic_slice_in_dim(slot_len, lax.axis_index("gx") * rows_dev, rows_dev, 0)
    qkv_cols = w_qkv.shape[1]
    blocks = (gx_size, requests // gx_size, attn_slot.shape[1])
    partial = jnp.concatenate(
        [
            jnp.einsum(
                "sbk,kn->sbn", attn_slot.reshape(blocks), w_qkv, preferred_element_type=jnp.float32
            ),
            jnp.einsum(
                "sbk,kn->sbn", mlp_slot.reshape(blocks), w_up, preferred_element_type=jnp.float32
            ),
        ],
        axis=2,
    )
    reduced = jnp.sum(lax.all_to_all(partial, "gx", 0, 0, tiled=False), axis=0)
    qkv = reduced[:, :qkv_cols] + b_qkv
    up = reduced[:, qkv_cols:] + b_up
    qkv = qkv.reshape(rows_dev, heads_dev, 3, HD)
    position = my_len - 1
    query = rotate(qkv[:, :, 0], position).astype(jnp.bfloat16)
    new_key = rotate(qkv[:, :, 1], position).astype(jnp.bfloat16)
    new_value = qkv[:, :, 2].astype(jnp.bfloat16)
    old_scores, valid = block_scores(query, key_cache, my_len)
    fresh = jnp.einsum(
        "shd,shd->sh", query, new_key, preferred_element_type=jnp.float32
    ) * HD ** (-0.5)
    places = lax.iota(jnp.int32, key_cache.shape[2])
    scores = jnp.where(
        places[None, None, :] == position[:, None, None], fresh[:, :, None], old_scores
    )
    top_score = jnp.max(scores, axis=2)
    weights = jnp.where(valid, jnp.exp(scores - top_score[:, :, None]), 0.0)
    total = jnp.sum(weights, axis=2)
    weights_low = weights.astype(jnp.bfloat16)
    at_new = places[None, None, :] == position[:, None, None]
    weighted = jnp.einsum(
        "shp,shpd->shd",
        jnp.where(at_new, jnp.zeros_like(weights_low), weights_low),
        value_cache,
        preferred_element_type=jnp.float32,
    ) + jnp.sum(
        jnp.where(at_new, weights_low, jnp.zeros_like(weights_low)).astype(jnp.float32), axis=2
    )[:, :, None] * new_value.astype(jnp.float32)
    attended = (weighted / total[:, :, None]).astype(jnp.bfloat16).reshape(rows_dev, heads_dev * HD)
    hidden = jax.nn.gelu(up, approximate=False).astype(jnp.bfloat16)
    at_row = (places[None, :] == position[:, None])[:, None, :, None]
    new_keys = jnp.where(at_row, new_key[:, :, None, :], key_cache)
    new_values = jnp.where(at_row, new_value[:, :, None, :], value_cache)
    both = jnp.concatenate([attended, hidden], axis=1)
    gathered = lax.all_to_all(
        jnp.broadcast_to(both[None], (gx_size,) + both.shape), "gx", 0, 0, tiled=False
    )
    slot_part = jnp.einsum(
        "sbk,kn->sbn", gathered, w_both, preferred_element_type=jnp.float32
    ).reshape(requests, w_out.shape[1])
    branches = pair_sum(slot_part, "gy", gy_pairs(gy_size))
    branches = jnp.dot(to_request, branches, precision=lax.Precision.HIGHEST)
    hidden_out = (wide_in + branches + b_out + b_down).astype(jnp.bfloat16)
    return (hidden_out, new_keys, new_values)


def solution(mesh):
    body = functools.partial(layer, gx_size=mesh.shape["gx"], gy_size=mesh.shape["gy"])
    return jax.shard_map(
        body,
        mesh=mesh,
        in_specs=(
            P(None, "gx"),
            P("gx"),
            P("gx"),
            P("gx"),
            P("gx"),
            P("gx", "gy"),
            P("gy"),
            P("gy", "gx"),
            P("gx"),
            P("gx", "gy"),
            P("gy"),
            P("gy", "gx"),
            P("gx"),
            P("gx", "gy", None, None),
            P("gx", "gy", None, None),
            P(),
            P(),
        ),
        out_specs=(P(None, "gx"), P("gx", "gy", None, None), P("gx", "gy", None, None)),
        check_vma=False,
    )
```

```python
import functools

import jax
import jax.numpy as jnp
from jax import lax
from jax.sharding import PartitionSpec as P


D = 5120
HD = 128
ROT = 32


def rotate(tensor, position):
    half_rot = ROT // 2
    frequency = 10000.0 ** (-2.0 * jnp.arange(half_rot, dtype=jnp.float32) / ROT)
    angle = position.astype(jnp.float32)[:, None, None] * frequency
    cosine = jnp.cos(angle)
    sine = jnp.sin(angle)
    first_half = tensor[..., :half_rot]
    second_half = tensor[..., half_rot:ROT]
    return jnp.concatenate(
        [
            first_half * cosine - second_half * sine,
            second_half * cosine + first_half * sine,
            tensor[..., ROT:],
        ],
        axis=-1,
    )


def block_scores(query, keys, my_len):
    span_len = keys.shape[2]
    scores = jnp.einsum("shd,shpd->shp", query, keys, preferred_element_type=jnp.float32) * HD ** (
        -0.5
    )
    places = lax.iota(jnp.int32, span_len)
    valid = places[None, None, :] < my_len[:, None, None]
    return (jnp.where(valid, scores, -1e30), valid)


def xor_pairs(size, bit):
    return [(i, i ^ (1 << bit)) for i in range(size)]


def exchange_sum(x, axis, size):
    spread = jnp.broadcast_to(x[None], (size,) + x.shape)
    return jnp.sum(lax.all_to_all(spread, axis, 0, 0, tiled=False), axis=0)


def pair_sum(x, axis, rounds):
    for pairs in rounds:
        x = x + lax.ppermute(x, axis, pairs)
    return x


def gy_pairs(size):
    rounds = [xor_pairs(size, bit) for bit in range(size.bit_length() - 1)]
    if size == 8:
        rounds[2] = [(i, (3 - i // 2) * 2 + i % 2) for i in range(size)]
    return rounds


def layer(
    hidden_in,
    norm1_gain,
    norm1_bias,
    norm2_gain,
    norm2_bias,
    w_qkv,
    b_qkv,
    w_out,
    b_out,
    w_up,
    b_up,
    w_down,
    b_down,
    key_cache,
    value_cache,
    lengths,
    assignment,
    gx_size,
    gy_size,
):
    requests = hidden_in.shape[0]
    rows_dev = key_cache.shape[0]
    heads_dev = key_cache.shape[1]
    wide_in = hidden_in.astype(jnp.float32)
    stats = exchange_sum(
        jnp.concatenate([jnp.sum(wide_in, axis=1), jnp.sum(wide_in * wide_in, axis=1)]),
        "gx",
        gx_size,
    ).reshape(2, requests)
    slot_ids = lax.iota(jnp.int32, requests)
    matches = assignment[:, None] == slot_ids[None, :]
    to_request = matches.astype(jnp.float32)
    x_slot = jnp.dot(matches.T.astype(jnp.bfloat16), hidden_in, preferred_element_type=jnp.float32)
    w_both = jnp.concatenate([w_out, w_down], axis=0)
    stats = jnp.sum(jnp.where(matches[None], stats[:, :, None], 0.0), axis=1)
    sum_rows, sum_squares = stats[0], stats[1]
    row_mean = sum_rows / D
    row_var = sum_squares / D - row_mean * row_mean
    normed = (x_slot - row_mean[:, None]) * lax.rsqrt(row_var + 1e-05)[:, None]
    attn_slot = (normed * norm1_gain + norm1_bias).astype(jnp.bfloat16)
    mlp_slot = (normed * norm2_gain + norm2_bias).astype(jnp.bfloat16)
    slot_len = jnp.sum(jnp.where(matches, lengths[:, None], 0), axis=0)
    my_len = lax.dynamic_slice_in_dim(slot_len, lax.axis_index("gx") * rows_dev, rows_dev, 0)
    qkv_cols = w_qkv.shape[1]
    blocks = (gx_size, requests // gx_size, attn_slot.shape[1])
    partial = jnp.concatenate(
        [
            jnp.einsum(
                "sbk,kn->sbn", attn_slot.reshape(blocks), w_qkv, preferred_element_type=jnp.float32
            ),
            jnp.einsum(
                "sbk,kn->sbn", mlp_slot.reshape(blocks), w_up, preferred_element_type=jnp.float32
            ),
        ],
        axis=2,
    )
    received = lax.all_to_all(partial, "gx", 0, 0, tiled=False)
    qkv = jnp.sum(received[:, :, :qkv_cols], axis=0) + b_qkv
    up = jnp.sum(received[:, :, qkv_cols:], axis=0) + b_up
    qkv = qkv.reshape(rows_dev, heads_dev, 3, HD)
    position = my_len - 1
    query = rotate(qkv[:, :, 0], position).astype(jnp.bfloat16)
    new_key = rotate(qkv[:, :, 1], position).astype(jnp.bfloat16)
    new_value = qkv[:, :, 2].astype(jnp.bfloat16)
    old_scores, valid = block_scores(query, key_cache, my_len)
    fresh = jnp.einsum(
        "shd,shd->sh", query, new_key, preferred_element_type=jnp.float32
    ) * HD ** (-0.5)
    places = lax.iota(jnp.int32, key_cache.shape[2])
    scores = jnp.where(
        places[None, None, :] == position[:, None, None], fresh[:, :, None], old_scores
    )
    top_score = jnp.max(scores, axis=2)
    weights = jnp.where(valid, jnp.exp(scores - top_score[:, :, None]), 0.0)
    total = jnp.sum(weights, axis=2)
    weights_low = weights.astype(jnp.bfloat16)
    at_new = places[None, None, :] == position[:, None, None]
    weighted = jnp.einsum(
        "shp,shpd->shd",
        jnp.where(at_new, jnp.zeros_like(weights_low), weights_low),
        value_cache,
        preferred_element_type=jnp.float32,
    ) + jnp.sum(
        jnp.where(at_new, weights_low, jnp.zeros_like(weights_low)).astype(jnp.float32), axis=2
    )[:, :, None] * new_value.astype(jnp.float32)
    attended = (weighted / total[:, :, None]).astype(jnp.bfloat16).reshape(rows_dev, heads_dev * HD)
    hidden = jax.nn.gelu(up, approximate=False).astype(jnp.bfloat16)
    at_row = (places[None, :] == position[:, None])[:, None, :, None]
    new_keys = jnp.where(at_row, new_key[:, :, None, :], key_cache)
    new_values = jnp.where(at_row, new_value[:, :, None, :], value_cache)
    both = jnp.concatenate([attended, hidden], axis=1)
    gathered = lax.all_to_all(
        jnp.broadcast_to(both[None], (gx_size,) + both.shape), "gx", 0, 0, tiled=False
    )
    slot_part = jnp.einsum(
        "sbk,kn->sbn", gathered, w_both, preferred_element_type=jnp.float32
    ).reshape(requests, w_out.shape[1])
    branches = pair_sum(slot_part, "gy", gy_pairs(gy_size))
    branches = jnp.dot(to_request, branches, precision=lax.Precision.HIGHEST)
    hidden_out = (wide_in + branches + b_out + b_down).astype(jnp.bfloat16)
    return (hidden_out, new_keys, new_values)


def solution(mesh):
    body = functools.partial(layer, gx_size=mesh.shape["gx"], gy_size=mesh.shape["gy"])
    return jax.shard_map(
        body,
        mesh=mesh,
        in_specs=(
            P(None, "gx"),
            P("gx"),
            P("gx"),
            P("gx"),
            P("gx"),
            P("gx", "gy"),
            P("gy"),
            P("gy", "gx"),
            P("gx"),
            P("gx", "gy"),
            P("gy"),
            P("gy", "gx"),
            P("gx"),
            P("gx", "gy", None, None),
            P("gx", "gy", None, None),
            P(),
            P(),
        ),
        out_specs=(P(None, "gx"), P("gx", "gy", None, None), P("gx", "gy", None, None)),
        check_vma=False,
    )
```

```python
import functools

import jax
import jax.numpy as jnp
from jax import lax
from jax.sharding import PartitionSpec as P


D = 5120
HD = 128
ROT = 32


def rotate(tensor, position):
    half_rot = ROT // 2
    frequency = 10000.0 ** (-2.0 * jnp.arange(half_rot, dtype=jnp.float32) / ROT)
    angle = position.astype(jnp.float32)[:, None, None] * frequency
    cosine = jnp.cos(angle)
    sine = jnp.sin(angle)
    first_half = tensor[..., :half_rot]
    second_half = tensor[..., half_rot:ROT]
    return jnp.concatenate(
        [
            first_half * cosine - second_half * sine,
            second_half * cosine + first_half * sine,
            tensor[..., ROT:],
        ],
        axis=-1,
    )


def block_scores(query, keys, my_len):
    span_len = keys.shape[2]
    scores = jnp.einsum("shd,shpd->shp", query, keys, preferred_element_type=jnp.float32) * HD ** (
        -0.5
    )
    places = lax.iota(jnp.int32, span_len)
    valid = places[None, None, :] < my_len[:, None, None]
    return (jnp.where(valid, scores, -1e30), valid)


def xor_pairs(size, bit):
    return [(i, i ^ (1 << bit)) for i in range(size)]


def pair_sum(x, axis, rounds):
    for pairs in rounds:
        x = x + lax.ppermute(x, axis, pairs)
    return x


def gy_pairs(size):
    rounds = [xor_pairs(size, bit) for bit in range(size.bit_length() - 1)]
    if size == 8:
        rounds[2] = [(i, (3 - i // 2) * 2 + i % 2) for i in range(size)]
    return rounds


def layer(
    hidden_in,
    norm1_gain,
    norm1_bias,
    norm2_gain,
    norm2_bias,
    w_qkv,
    b_qkv,
    w_out,
    b_out,
    w_up,
    b_up,
    w_down,
    b_down,
    key_cache,
    value_cache,
    lengths,
    assignment,
    gx_size,
    gy_size,
):
    requests = hidden_in.shape[0]
    rows_dev = key_cache.shape[0]
    heads_dev = key_cache.shape[1]
    wide_in = hidden_in.astype(jnp.float32)
    spread = jnp.broadcast_to(
        jnp.concatenate([wide_in, wide_in * wide_in], axis=0)[None],
        (gx_size, 2 * requests, wide_in.shape[1]),
    )
    stats = jnp.sum(
        lax.all_to_all(jnp.sum(spread, axis=2), "gx", 0, 0, tiled=False), axis=0
    ).reshape(2, requests)
    slot_ids = lax.iota(jnp.int32, requests)
    matches = assignment[:, None] == slot_ids[None, :]
    to_request = matches.astype(jnp.float32)
    x_slot = jnp.dot(matches.T.astype(jnp.bfloat16), hidden_in, preferred_element_type=jnp.float32)
    w_both = jnp.concatenate([w_out, w_down], axis=0)
    stats = jnp.sum(jnp.where(matches[None], stats[:, :, None], 0.0), axis=1)
    sum_rows, sum_squares = stats[0], stats[1]
    row_mean = sum_rows / D
    row_var = sum_squares / D - row_mean * row_mean
    normed = (x_slot - row_mean[:, None]) * lax.rsqrt(row_var + 1e-05)[:, None]
    attn_slot = (normed * norm1_gain + norm1_bias).astype(jnp.bfloat16)
    mlp_slot = (normed * norm2_gain + norm2_bias).astype(jnp.bfloat16)
    slot_len = jnp.sum(jnp.where(matches, lengths[:, None], 0), axis=0)
    my_len = lax.dynamic_slice_in_dim(slot_len, lax.axis_index("gx") * rows_dev, rows_dev, 0)
    qkv_cols = w_qkv.shape[1]
    blocks = (gx_size, requests // gx_size, attn_slot.shape[1])
    partial = jnp.concatenate(
        [
            jnp.einsum(
                "sbk,kn->sbn", attn_slot.reshape(blocks), w_qkv, preferred_element_type=jnp.float32
            ),
            jnp.einsum(
                "sbk,kn->sbn", mlp_slot.reshape(blocks), w_up, preferred_element_type=jnp.float32
            ),
        ],
        axis=2,
    )
    reduced = jnp.sum(lax.all_to_all(partial, "gx", 0, 0, tiled=False), axis=0)
    qkv = reduced[:, :qkv_cols] + b_qkv
    up = reduced[:, qkv_cols:] + b_up
    qkv = qkv.reshape(rows_dev, heads_dev, 3, HD)
    position = my_len - 1
    query = rotate(qkv[:, :, 0], position).astype(jnp.bfloat16)
    new_key = rotate(qkv[:, :, 1], position).astype(jnp.bfloat16)
    new_value = qkv[:, :, 2].astype(jnp.bfloat16)
    old_scores, valid = block_scores(query, key_cache, my_len)
    fresh = jnp.einsum(
        "shd,shd->sh", query, new_key, preferred_element_type=jnp.float32
    ) * HD ** (-0.5)
    places = lax.iota(jnp.int32, key_cache.shape[2])
    scores = jnp.where(
        places[None, None, :] == position[:, None, None], fresh[:, :, None], old_scores
    )
    top_score = jnp.max(scores, axis=2)
    weights = jnp.where(valid, jnp.exp(scores - top_score[:, :, None]), 0.0)
    total = jnp.sum(weights, axis=2)
    weights_low = weights.astype(jnp.bfloat16)
    at_new = places[None, None, :] == position[:, None, None]
    weighted = jnp.einsum(
        "shp,shpd->shd",
        jnp.where(at_new, jnp.zeros_like(weights_low), weights_low),
        value_cache,
        preferred_element_type=jnp.float32,
    ) + jnp.sum(
        jnp.where(at_new, weights_low, jnp.zeros_like(weights_low)).astype(jnp.float32), axis=2
    )[:, :, None] * new_value.astype(jnp.float32)
    attended = (weighted / total[:, :, None]).astype(jnp.bfloat16).reshape(rows_dev, heads_dev * HD)
    hidden = jax.nn.gelu(up, approximate=False).astype(jnp.bfloat16)
    at_row = (places[None, :] == position[:, None])[:, None, :, None]
    new_keys = jnp.where(at_row, new_key[:, :, None, :], key_cache)
    new_values = jnp.where(at_row, new_value[:, :, None, :], value_cache)
    both = jnp.concatenate([attended, hidden], axis=1)
    gathered = lax.all_to_all(
        jnp.broadcast_to(both[None], (gx_size,) + both.shape), "gx", 0, 0, tiled=False
    )
    slot_part = jnp.einsum(
        "sbk,kn->sbn", gathered, w_both, preferred_element_type=jnp.float32
    ).reshape(requests, w_out.shape[1])
    branches = pair_sum(slot_part, "gy", gy_pairs(gy_size))
    branches = jnp.dot(to_request, branches, precision=lax.Precision.HIGHEST)
    hidden_out = (wide_in + branches + b_out + b_down).astype(jnp.bfloat16)
    return (hidden_out, new_keys, new_values)


def solution(mesh):
    body = functools.partial(layer, gx_size=mesh.shape["gx"], gy_size=mesh.shape["gy"])
    return jax.shard_map(
        body,
        mesh=mesh,
        in_specs=(
            P(None, "gx"),
            P("gx"),
            P("gx"),
            P("gx"),
            P("gx"),
            P("gx", "gy"),
            P("gy"),
            P("gy", "gx"),
            P("gx"),
            P("gx", "gy"),
            P("gy"),
            P("gy", "gx"),
            P("gx"),
            P("gx", "gy", None, None),
            P("gx", "gy", None, None),
            P(),
            P(),
        ),
        out_specs=(P(None, "gx"), P("gx", "gy", None, None), P("gx", "gy", None, None)),
        check_vma=False,
    )
```

```python
import functools

import jax
import jax.numpy as jnp
from jax import lax
from jax.sharding import PartitionSpec as P


D = 5120
HD = 128
ROT = 32


def rotate(tensor, position):
    half_rot = ROT // 2
    frequency = 10000.0 ** (-2.0 * jnp.arange(half_rot, dtype=jnp.float32) / ROT)
    angle = position.astype(jnp.float32)[:, None, None] * frequency
    cosine = jnp.cos(angle)
    sine = jnp.sin(angle)
    first_half = tensor[..., :half_rot]
    second_half = tensor[..., half_rot:ROT]
    return jnp.concatenate(
        [
            first_half * cosine - second_half * sine,
            second_half * cosine + first_half * sine,
            tensor[..., ROT:],
        ],
        axis=-1,
    )


def block_scores(query, keys, my_len):
    span_len = keys.shape[2]
    scores = jnp.einsum("shd,shpd->shp", query, keys, preferred_element_type=jnp.float32) * HD ** (
        -0.5
    )
    places = lax.iota(jnp.int32, span_len)
    valid = places[None, None, :] < my_len[:, None, None]
    return (jnp.where(valid, scores, -1e30), valid)


def xor_pairs(size, bit):
    return [(i, i ^ (1 << bit)) for i in range(size)]


def exchange_sum(x, axis, size):
    spread = jnp.broadcast_to(x[None], (size,) + x.shape)
    return jnp.sum(lax.all_to_all(spread, axis, 0, 0, tiled=False), axis=0)


def pair_sum(x, axis, rounds):
    for pairs in rounds:
        x = x + lax.ppermute(x, axis, pairs)
    return x


def gy_pairs(size):
    rounds = [xor_pairs(size, bit) for bit in range(size.bit_length() - 1)]
    if size == 8:
        rounds[2] = [(i, (3 - i // 2) * 2 + i % 2) for i in range(size)]
    return rounds


def layer(
    hidden_in,
    norm1_gain,
    norm1_bias,
    norm2_gain,
    norm2_bias,
    w_qkv,
    b_qkv,
    w_out,
    b_out,
    w_up,
    b_up,
    w_down,
    b_down,
    key_cache,
    value_cache,
    lengths,
    assignment,
    gx_size,
    gy_size,
):
    requests = hidden_in.shape[0]
    rows_dev = key_cache.shape[0]
    heads_dev = key_cache.shape[1]
    wide_in = hidden_in.astype(jnp.float32)
    stats = exchange_sum(
        jnp.concatenate([jnp.sum(wide_in, axis=1), jnp.sum(wide_in * wide_in, axis=1)]),
        "gx",
        gx_size,
    ).reshape(2, requests)
    slot_ids = lax.iota(jnp.int32, requests)
    matches = assignment[:, None] == slot_ids[None, :]
    to_request = matches.astype(jnp.float32)
    x_slot = jnp.dot(matches.T.astype(jnp.bfloat16), hidden_in, preferred_element_type=jnp.float32)
    w_both = jnp.concatenate([w_out, w_down], axis=0)
    stats = jnp.sum(jnp.where(matches[None], stats[:, :, None], 0.0), axis=1)
    sum_rows, sum_squares = stats[0], stats[1]
    row_mean = sum_rows / D
    row_var = sum_squares / D - row_mean * row_mean
    normed = (x_slot - row_mean[:, None]) * lax.rsqrt(row_var + 1e-05)[:, None]
    attn_slot = (normed * norm1_gain + norm1_bias).astype(jnp.bfloat16)
    mlp_slot = (normed * norm2_gain + norm2_bias).astype(jnp.bfloat16)
    slot_len = jnp.sum(jnp.where(matches, lengths[:, None], 0), axis=0)
    my_len = lax.dynamic_slice_in_dim(slot_len, lax.axis_index("gx") * rows_dev, rows_dev, 0)
    qkv_cols = w_qkv.shape[1]
    blocks = (gx_size, requests // gx_size, attn_slot.shape[1])
    partial = jnp.concatenate(
        [
            jnp.einsum(
                "sbk,kn->sbn", attn_slot.reshape(blocks), w_qkv, preferred_element_type=jnp.float32
            ),
            jnp.einsum(
                "sbk,kn->sbn", mlp_slot.reshape(blocks), w_up, preferred_element_type=jnp.float32
            ),
        ],
        axis=2,
    )
    reduced = jnp.sum(lax.all_to_all(partial, "gx", 0, 0, tiled=False), axis=0)
    qkv = reduced[:, :qkv_cols] + b_qkv
    up = reduced[:, qkv_cols:] + b_up
    qkv = qkv.reshape(rows_dev, heads_dev, 3, HD)
    position = my_len - 1
    query = rotate(qkv[:, :, 0], position).astype(jnp.bfloat16)
    new_key = rotate(qkv[:, :, 1], position).astype(jnp.bfloat16)
    new_value = qkv[:, :, 2].astype(jnp.bfloat16)
    old_scores, valid = block_scores(query, key_cache, my_len)
    fresh = jnp.einsum(
        "shd,shd->sh", query, new_key, preferred_element_type=jnp.float32
    ) * HD ** (-0.5)
    places = lax.iota(jnp.int32, key_cache.shape[2])
    scores = jnp.where(
        places[None, None, :] == position[:, None, None], fresh[:, :, None], old_scores
    )
    top_score = jnp.max(scores, axis=2)
    weights = jnp.where(valid, jnp.exp(scores - top_score[:, :, None]), 0.0)
    total = jnp.sum(weights, axis=2)
    weights_low = weights.astype(jnp.bfloat16)
    at_new = places[None, None, :] == position[:, None, None]
    weighted = jnp.einsum(
        "shp,shpd->shd",
        jnp.where(at_new, jnp.zeros_like(weights_low), weights_low),
        value_cache,
        preferred_element_type=jnp.float32,
    ) + jnp.sum(
        jnp.where(at_new, weights_low, jnp.zeros_like(weights_low)).astype(jnp.float32), axis=2
    )[:, :, None] * new_value.astype(jnp.float32)
    attended = (weighted / total[:, :, None]).astype(jnp.bfloat16).reshape(rows_dev, heads_dev * HD)
    hidden = jax.nn.gelu(up, approximate=False).astype(jnp.bfloat16)
    at_row = (places[None, :] == position[:, None])[:, None, :, None]
    new_keys = jnp.where(at_row, new_key[:, :, None, :], key_cache)
    new_values = jnp.where(at_row, new_value[:, :, None, :], value_cache)
    both = jnp.concatenate([attended, hidden], axis=1)
    gathered = lax.all_to_all(
        jnp.broadcast_to(both[None], (gx_size,) + both.shape), "gx", 0, 0, tiled=False
    )
    request_rows = jnp.dot(
        matches.astype(jnp.bfloat16),
        gathered.reshape(requests, gathered.shape[2]),
        preferred_element_type=jnp.float32,
    ).astype(jnp.bfloat16)
    slot_part = jnp.dot(request_rows, w_both, preferred_element_type=jnp.float32)
    branches = pair_sum(slot_part, "gy", gy_pairs(gy_size))
    hidden_out = (wide_in + branches + b_out + b_down).astype(jnp.bfloat16)
    return (hidden_out, new_keys, new_values)


def solution(mesh):
    body = functools.partial(layer, gx_size=mesh.shape["gx"], gy_size=mesh.shape["gy"])
    return jax.shard_map(
        body,
        mesh=mesh,
        in_specs=(
            P(None, "gx"),
            P("gx"),
            P("gx"),
            P("gx"),
            P("gx"),
            P("gx", "gy"),
            P("gy"),
            P("gy", "gx"),
            P("gx"),
            P("gx", "gy"),
            P("gy"),
            P("gy", "gx"),
            P("gx"),
            P("gx", "gy", None, None),
            P("gx", "gy", None, None),
            P(),
            P(),
        ),
        out_specs=(P(None, "gx"), P("gx", "gy", None, None), P("gx", "gy", None, None)),
        check_vma=False,
    )
```
